32 devices in a mesh: cells: 32 (over z, y, x, core).
Axes of the slice: x: 2, y: 2, z: 4, core: 2. Of those that a mesh axis runs over, the one named last changes fastest.
Arguments:
- concentration: float32 [9, 256, 4096], P(None, None, 'cells'), may hold values from 0.05 to 4
- flux_weight: float32 [8, 9, 4096], P(None, None, 'cells'), may hold values from 0.01 to 0.08
- vertical_mixing: float32 [8, 4096], P(None, 'cells'), may hold values from 0.02 to 0.15
- deposition: float32 [9, 4096], P(None, 'cells'), may hold values from 0.02 to 0.3
- halo_index: int32 [8, 4096], P(None, 'cells'), may hold values from 0 to 639, as said below
- send_cells: int32 [32, 32, 16], P('cells'), may hold values from 0 to 127, as said below
- live_count: int32 [32], P('cells'), may hold values from 32 to 128, as said below
Outputs:
- advanced: float32 [9, 256, 4096], P(None, None, 'cells')
The draws below stay inside these ranges and needn't reach their ends.
Inputs may be any that keep to these rules, and one draw needn't show every extreme that they name: Device d's live cells are its slots 0 to live_count[d] - 1; some device is full in every draw. send_cells[d, p, h] is a live slot of device d. `halo_index`: every entry of a live cell of device d is a live slot of d below 128, or 128 + p * 16 + h for a sender p equal to d - 2, d - 1, d + 1 or d + 2 within the axis, or to (d + 16) mod 32.
All inputs are finite; a program needn't handle non-finite values.
Results may differ from the reference program's by a relative error of at most 0.00002.
Values sent between devices are 32-bit elements; how exact they have to be, the bound alone decides.
No kernel may reach another device: no remote copies, remote signals or barrier semaphores. Data moves between devices by JAX's collectives and lax.ppermute only.
A program may use at most 128 MiB of HBM per device.

```python
import math
import jax
import jax.numpy as jnp

CAP = 128
LEV = 9
PULSES = 256
NBR = 8
HSLOT = 16
STEPS = 2
CELLS = 4096
N_CELLS = 32


def live_counts(key):
    counted = jax.random.randint(jax.random.fold_in(key, 11), (N_CELLS,), CAP // 4, CAP + 1)
    fullest = jax.random.randint(jax.random.fold_in(key, 12), (), 0, N_CELLS)
    return jnp.where(jnp.arange(N_CELLS) == fullest, CAP, counted).astype(jnp.int32)


def draw_live_count(key, part):
    return live_counts(key)


def draw_send_cells(key, part):
    living = live_counts(key)
    raw_bits = jax.random.randint(jax.random.fold_in(key, 21), (N_CELLS, N_CELLS, HSLOT), 0, 2 ** 30)
    picked = raw_bits % living[:, None, None]
    first = jnp.arange(HSLOT, dtype=jnp.int32)[None, None, :] == 0
    return jnp.where(first, living[:, None, None] - 1, picked).astype(jnp.int32)


def draw_halo_index(key, part):
    living = live_counts(key)
    overall = N_CELLS * CAP
    holder = jnp.arange(overall, dtype=jnp.int32) // CAP
    raw_bits = jax.random.randint(jax.random.fold_in(key, 31), (NBR, overall), 0, 2 ** 30)
    locally = raw_bits % living[holder][None, :]
    picked = jax.random.randint(jax.random.fold_in(key, 32), (NBR, overall), 0, 16)
    offsets = jnp.array([1, -1, 2, -2], dtype=jnp.int32)
    nearer = holder[None, :] + offsets[jnp.clip(picked, 0, 3)]
    sender = jnp.where(picked == 4, (holder[None, :] + N_CELLS // 2) % N_CELLS, nearer)
    usable = (picked < 5) & (sender >= 0) & (sender < N_CELLS)
    place_in = jax.random.randint(jax.random.fold_in(key, 33), (NBR, overall), 0, HSLOT)
    remote = CAP + sender * HSLOT + place_in
    chosen = jnp.where(usable, remote, locally).astype(jnp.int32)
    return chosen.at[0, (N_CELLS - 2) * CAP].set(CAP + N_CELLS * HSLOT - 1)


def steps_of(stream_key, extent, shards, low, top_value):
    factor_of, own = 1.0, jax.random.fold_in(stream_key, 6)
    for dim, blocks in shards:
        heights = jnp.exp(jax.random.uniform(jax.random.fold_in(own, dim), (blocks,), jnp.float32, low / len(shards), top_value / len(shards)))
        factor_of = factor_of * jnp.repeat(heights, extent[dim] // blocks).reshape([-1 if axis == dim else 1 for axis in range(len(extent))])
    return factor_of


def setup_inputs(seed: int = 0) -> dict:
    streams_of = jax.random.split(jax.random.key(seed), 8)
    concentration = jnp.clip(jnp.exp(math.log(4.0) - 4.3820266 * jax.random.uniform(streams_of[0], (LEV, PULSES, CELLS), jnp.float32) ** steps_of(streams_of[0], (LEV, PULSES, CELLS), ((2, 32),), -0.2, 0.2)), 0.05, 4.0)
    flux_weight = jnp.clip(jnp.exp(math.log(0.08) - 2.0794415 * jax.random.uniform(streams_of[1], (NBR, LEV, CELLS), jnp.float32) ** steps_of(streams_of[1], (NBR, LEV, CELLS), ((2, 32),), -0.2, 0.2)), 0.01, 0.08)
    vertical_mixing = jnp.clip(jnp.exp(math.log(0.15) - 2.014903 * jax.random.uniform(streams_of[2], (LEV - 1, CELLS), jnp.float32) ** steps_of(streams_of[2], (LEV - 1, CELLS), ((1, 32),), -0.2, 0.2)), 0.02, 0.15)
    deposition = jnp.clip(jnp.exp(math.log(0.3) - 2.7080503 * jax.random.uniform(streams_of[3], (LEV, CELLS), jnp.float32) ** steps_of(streams_of[3], (LEV, CELLS), ((1, 32),), -0.2, 0.2)), 0.02, 0.3)
    halo_index = draw_halo_index(jax.random.fold_in(streams_of[7], 71), 0)
    send_cells = draw_send_cells(jax.random.fold_in(streams_of[7], 71), 0)
    live_count = draw_live_count(jax.random.fold_in(streams_of[7], 71), 0)
    return dict(concentration=concentration, flux_weight=flux_weight, vertical_mixing=vertical_mixing, deposition=deposition, halo_index=halo_index, send_cells=send_cells, live_count=live_count)


def reference(concentration, flux_weight, vertical_mixing, deposition, halo_index, send_cells, live_count):
    overall = N_CELLS * CAP
    numbers = jnp.arange(overall, dtype=jnp.int32)
    holder = (numbers // CAP).astype(jnp.int32)
    living = (numbers % CAP) < live_count[holder]
    beyond = halo_index - CAP
    sender = jnp.clip(beyond // HSLOT, 0, N_CELLS - 1).astype(jnp.int32)
    place_in = (beyond % HSLOT).astype(jnp.int32)
    listing = send_cells.reshape(-1)
    remote = sender * CAP + listing[((sender * N_CELLS + holder[None, :]) * HSLOT + place_in).astype(jnp.int32)]
    source = jnp.where(beyond >= 0, remote, holder[None, :] * CAP + halo_index).astype(jnp.int32)
    values = concentration
    for sweep in range(STEPS):
        flat_values = values.reshape(LEV * PULSES, overall)
        summed = jnp.zeros_like(values)
        for neighbour in range(NBR):
            nearby = flat_values[:, source[neighbour]].reshape(LEV, PULSES, overall)
            summed = summed + flux_weight[neighbour][:, None, :] * (nearby - values)
        upward = vertical_mixing[:, None, :] * (values[1:] - values[:-1])
        nothing = jnp.zeros_like(values[:1])
        vertical = jnp.concatenate([upward, nothing], axis=0) - jnp.concatenate([nothing, upward], axis=0)
        values = jnp.where(living[None, None, :], (values + summed + vertical) * (1.0 - deposition[:, None, :]), 0.0)
    return values
```

```python
import jax
import jax.numpy as jnp
from jax import lax
from jax.sharding import PartitionSpec as P

STEPS = 2
HIGHEST = lax.Precision.HIGHEST


def peer_shifts(n):
    return (1, -1, 2, -2, n // 2)


def permutation(n, shift):
    if shift == n // 2:
        return [(p, (p + shift) % n) for p in range(n)]
    return [(p, p + shift) for p in range(n) if 0 <= p + shift < n]


def per_device(
    n, concentration, flux_weight, vertical_mixing, deposition, halo_index, send_cells, live_count
):
    levels, pulses, capacity = concentration.shape
    hslot = send_cells.shape[2]
    shifts = peer_shifts(n)
    groups = len(shifts)
    me = lax.axis_index("cells")
    f32 = jnp.float32

    peers = (me + jnp.array(shifts, dtype=jnp.int32)) % n
    picked = send_cells[0][peers].reshape(groups * hslot)
    select = (picked[:, None] == jnp.arange(capacity, dtype=jnp.int32)[None, :]).astype(f32)

    beyond = halo_index - capacity
    sender = beyond // hslot
    place = beyond % hslot
    shift = (me - sender) % n
    group = jnp.full(halo_index.shape, -1, dtype=jnp.int32)
    for g, s in enumerate(shifts):
        group = jnp.where(shift == s % n, g, group)
    local_col = jnp.where(beyond < 0, halo_index, -1)
    remote_col = jnp.where((beyond >= 0) & (group >= 0), group * hslot + place, -1)
    onehot_local = (local_col[:, None, :] == jnp.arange(capacity)[None, :, None]).astype(f32)
    onehot_remote = (
        remote_col[:, None, :] == jnp.arange(groups * hslot)[None, :, None]
    ).astype(f32)
    local_matrix = sum(
        flux_weight[k][:, None, :] * onehot_local[k][None] for k in range(flux_weight.shape[0])
    )
    remote_matrix = sum(
        flux_weight[k][:, None, :] * onehot_remote[k][None] for k in range(flux_weight.shape[0])
    )
    weight_sum = jnp.sum(flux_weight, axis=0)

    living = jnp.arange(capacity, dtype=jnp.int32) < live_count[0]
    keep = 1.0 - deposition

    values = concentration
    for sweep in range(STEPS):
        outgoing = jnp.einsum("sc,lqc->slq", select, values, precision=HIGHEST)
        outgoing = outgoing.reshape(groups, hslot, levels * pulses)
        incoming = jnp.stack(
            [
                lax.ppermute(outgoing[g], "cells", perm=permutation(n, s))
                for g, s in enumerate(shifts)
            ]
        ).reshape(groups * hslot, levels, pulses)
        near = jnp.einsum("lqs,lsc->lqc", values, local_matrix, precision=HIGHEST)
        far = jnp.einsum("slq,lsc->lqc", incoming, remote_matrix, precision=HIGHEST)
        summed = near + far - weight_sum[:, None, :] * values
        upward = vertical_mixing[:, None, :] * (values[1:] - values[:-1])
        nothing = jnp.zeros_like(values[:1])
        vertical = jnp.concatenate([upward, nothing], axis=0) - jnp.concatenate(
            [nothing, upward], axis=0
        )
        values = jnp.where(
            living[None, None, :], (values + summed + vertical) * keep[:, None, :], 0.0
        )
    return values


def solution(mesh):
    n = mesh.shape["cells"]
    in_specs = (
        P(None, None, "cells"),
        P(None, None, "cells"),
        P(None, "cells"),
        P(None, "cells"),
        P(None, "cells"),
        P("cells", None, None),
        P("cells"),
    )
    out_specs = P(None, None, "cells")

    def body(*args):
        return per_device(n, *args)

    return jax.shard_map(body, mesh=mesh, in_specs=in_specs, out_specs=out_specs, check_vma=False)
```

```python
import functools

import jax
import jax.numpy as jnp
from jax import lax
from jax.experimental import pallas as pl
from jax.sharding import PartitionSpec as P

STEPS = 2
HIGHEST = lax.Precision.HIGHEST
INTERPRET = False
NT = (((1,), (1,)), ((), ()))
TN = (((0,), (0,)), ((), ()))


def peer_shifts(n):
    return (n // 2, 1, -1, 2, -2)


def permutation(n, shift):
    if shift == n // 2:
        return [(p, (p + shift) % n) for p in range(n)]
    return [(p, p + shift) for p in range(n) if 0 <= p + shift < n]


def select_kernel(groups, hslot, pulses, values_ref, select_ref, *out_refs):
    select = select_ref[...]
    for level in range(values_ref.shape[0]):
        block = lax.dot_general(
            select, values_ref[level], NT, precision=HIGHEST, preferred_element_type=jnp.float32
        )
        for g in range(groups):
            out_refs[g][:, level * pulses : (level + 1) * pulses] = block[g * hslot : (g + 1) * hslot]


def gather_send(values, select, groups, hslot):
    levels, pulses, capacity = values.shape
    return pl.pallas_call(
        functools.partial(select_kernel, groups, hslot, pulses),
        out_shape=[jax.ShapeDtypeStruct((hslot, levels * pulses), jnp.float32)] * groups,
        interpret=INTERPRET,
        name="gather_send",
    )(values, select)


def local_kernel(values_ref, local_ref, weight_sum_ref, mixing_ref, out_ref):
    levels = values_ref.shape[0]
    for level in range(levels):
        v = values_ref[level]
        x = v - weight_sum_ref[level : level + 1, :] * v
        x = x + jnp.dot(
            v, local_ref[level], precision=HIGHEST, preferred_element_type=jnp.float32
        )
        if level + 1 < levels:
            x = x + mixing_ref[level : level + 1, :] * (values_ref[level + 1] - v)
        if level > 0:
            x = x - mixing_ref[level - 1 : level, :] * (v - values_ref[level - 1])
        out_ref[level] = x


def local_part(values, local_matrix, weight_sum, mixing):
    return pl.pallas_call(
        local_kernel,
        out_shape=jax.ShapeDtypeStruct(values.shape, jnp.float32),
        interpret=INTERPRET,
        name="local_part",
    )(values, local_matrix, weight_sum, mixing)


def finish_kernel(groups, hslot, pulses, send, *refs):
    partial_ref = refs[0]
    incoming = refs[1 : 1 + groups]
    remote_ref, keep_ref, living_ref, select_ref = refs[1 + groups : 5 + groups]
    out_ref = refs[5 + groups]
    send_refs = refs[6 + groups :]
    living = living_ref[...] > 0.5
    for level in range(partial_ref.shape[0]):
        columns = slice(level * pulses, (level + 1) * pulses)
        received = jnp.concatenate([incoming[g][:, columns] for g in range(groups)], axis=0)
        far = lax.dot_general(
            received, remote_ref[level], TN, precision=HIGHEST, preferred_element_type=jnp.float32
        )
        x = (partial_ref[level] + far) * keep_ref[level : level + 1, :]
        x = jnp.where(living, x, 0.0)
        out_ref[level] = x
        if send:
            block = lax.dot_general(
                select_ref[...], x, NT, precision=HIGHEST, preferred_element_type=jnp.float32
            )
            for g in range(groups):
                send_refs[g][:, columns] = block[g * hslot : (g + 1) * hslot]


def finish(partial, incoming, remote_matrix, keep, living, select, send):
    levels, pulses, capacity = partial.shape
    groups = len(incoming)
    hslot = incoming[0].shape[0]
    shapes = [jax.ShapeDtypeStruct(partial.shape, jnp.float32)]
    if send:
        shapes += [jax.ShapeDtypeStruct((hslot, levels * pulses), jnp.float32)] * groups
    outs = pl.pallas_call(
        functools.partial(finish_kernel, groups, hslot, pulses, send),
        out_shape=shapes,
        interpret=INTERPRET,
        name="finish_send" if send else "finish",
    )(partial, *incoming, remote_matrix, keep, living, select)
    return outs[0], outs[1:]


def per_device(
    n, concentration, flux_weight, vertical_mixing, deposition, halo_index, send_cells, live_count
):
    levels, pulses, capacity = concentration.shape
    hslot = send_cells.shape[2]
    nbr = flux_weight.shape[0]
    shifts = peer_shifts(n)
    groups = len(shifts)
    me = lax.axis_index("cells")
    f32 = jnp.float32

    peers = (me + jnp.array(shifts, dtype=jnp.int32)) % n
    picked = send_cells[0][peers].reshape(groups * hslot)
    select = (picked[:, None] == jnp.arange(capacity, dtype=jnp.int32)[None, :]).astype(f32)

    values = concentration
    outgoing = gather_send(values, select, groups, hslot)

    beyond = halo_index - capacity
    sender = beyond // hslot
    place = beyond % hslot
    shift = (me - sender) % n
    group = jnp.full(halo_index.shape, -1, dtype=jnp.int32)
    for g, s in enumerate(shifts):
        group = jnp.where(shift == s % n, g, group)
    local_col = jnp.where(beyond < 0, halo_index, -1)
    remote_col = jnp.where((beyond >= 0) & (group >= 0), group * hslot + place, -1)
    onehot_local = (local_col[:, None, :] == jnp.arange(capacity)[None, :, None]).astype(f32)
    onehot_remote = (
        remote_col[:, None, :] == jnp.arange(groups * hslot)[None, :, None]
    ).astype(f32)
    local_matrix = sum(flux_weight[k][:, None, :] * onehot_local[k][None] for k in range(nbr))
    remote_matrix = sum(flux_weight[k][:, None, :] * onehot_remote[k][None] for k in range(nbr))
    weight_sum = sum(flux_weight[k] for k in range(nbr))

    living = (jnp.arange(capacity, dtype=jnp.int32) < live_count[0]).astype(f32)[None, :]
    keep = 1.0 - deposition

    for sweep in range(STEPS):
        incoming = [
            lax.ppermute(outgoing[g], "cells", perm=permutation(n, s))
            for g, s in enumerate(shifts)
        ]
        partial = local_part(values, local_matrix, weight_sum, vertical_mixing)
        values, outgoing = finish(
            partial, incoming, remote_matrix, keep, living, select, sweep + 1 < STEPS
        )
    return values


def solution(mesh):
    n = mesh.shape["cells"]
    in_specs = (
        P(None, None, "cells"),
        P(None, None, "cells"),
        P(None, "cells"),
        P(None, "cells"),
        P(None, "cells"),
        P("cells", None, None),
        P("cells"),
    )
    out_specs = P(None, None, "cells")

    def body(*args):
        return per_device(n, *args)

    return jax.shard_map(body, mesh=mesh, in_specs=in_specs, out_specs=out_specs, check_vma=False)
```

```python
import functools

import jax
import numpy as np
import jax.numpy as jnp
from jax import lax
from jax.experimental import pallas as pl
from jax.sharding import PartitionSpec as P

STEPS = 2
HIGHEST = lax.Precision.HIGHEST
INTERPRET = False
NT = (((1,), (1,)), ((), ()))
TN = (((0,), (0,)), ((), ()))


def pairings(n):
    half = n // 2
    return (
        lambda d, xp: (d + half) % n,
        lambda d, xp: d ^ 1,
        lambda d, xp: xp.where(d % 2 == 1, d + 1, d - 1),
        lambda d, xp: xp.where(d % 4 < 2, d + 2, d - 2),
        lambda d, xp: xp.where(d % 4 < 2, d - 2, d + 2),
    )


def pair_list(n, partner):
    pairs = []
    for d in range(n):
        p = int(partner(d, np))
        if 0 <= p < n and p != d:
            pairs.append((d, p))
    return pairs


def select_kernel(groups, hslot, pulses, values_ref, select_ref, *out_refs):
    select = select_ref[...]
    for level in range(values_ref.shape[0]):
        block = lax.dot_general(
            select, values_ref[level], NT, precision=HIGHEST, preferred_element_type=jnp.float32
        )
        for g in range(groups):
            out_refs[g][:, level * pulses : (level + 1) * pulses] = block[g * hslot : (g + 1) * hslot]


def gather_send(values, select, groups, hslot):
    levels, pulses, capacity = values.shape
    return pl.pallas_call(
        functools.partial(select_kernel, groups, hslot, pulses),
        out_shape=[jax.ShapeDtypeStruct((hslot, levels * pulses), jnp.float32)] * groups,
        interpret=INTERPRET,
        name="gather_send",
    )(values, select)


def local_kernel(values_ref, local_ref, weight_sum_ref, mixing_ref, out_ref):
    levels = values_ref.shape[0]
    for level in range(levels):
        v = values_ref[level]
        x = v - weight_sum_ref[level : level + 1, :] * v
        x = x + jnp.dot(
            v, local_ref[level], precision=HIGHEST, preferred_element_type=jnp.float32
        )
        if level + 1 < levels:
            x = x + mixing_ref[level : level + 1, :] * (values_ref[level + 1] - v)
        if level > 0:
            x = x - mixing_ref[level - 1 : level, :] * (v - values_ref[level - 1])
        out_ref[level] = x


def local_part(values, local_matrix, weight_sum, mixing):
    return pl.pallas_call(
        local_kernel,
        out_shape=jax.ShapeDtypeStruct(values.shape, jnp.float32),
        interpret=INTERPRET,
        name="local_part",
    )(values, local_matrix, weight_sum, mixing)


def finish_kernel(groups, hslot, pulses, send, *refs):
    partial_ref = refs[0]
    incoming = refs[1 : 1 + groups]
    remote_ref, keep_ref, living_ref, select_ref = refs[1 + groups : 5 + groups]
    out_ref = refs[5 + groups]
    send_refs = refs[6 + groups :]
    living = living_ref[...] > 0.5
    for level in range(partial_ref.shape[0]):
        columns = slice(level * pulses, (level + 1) * pulses)
        received = jnp.concatenate([incoming[g][:, columns] for g in range(groups)], axis=0)
        far = lax.dot_general(
            received, remote_ref[level], TN, precision=HIGHEST, preferred_element_type=jnp.float32
        )
        x = (partial_ref[level] + far) * keep_ref[level : level + 1, :]
        x = jnp.where(living, x, 0.0)
        out_ref[level] = x
        if send:
            block = lax.dot_general(
                select_ref[...], x, NT, precision=HIGHEST, preferred_element_type=jnp.float32
            )
            for g in range(groups):
                send_refs[g][:, columns] = block[g * hslot : (g + 1) * hslot]


def finish(partial, incoming, remote_matrix, keep, living, select, send):
    levels, pulses, capacity = partial.shape
    groups = len(incoming)
    hslot = incoming[0].shape[0]
    shapes = [jax.ShapeDtypeStruct(partial.shape, jnp.float32)]
    if send:
        shapes += [jax.ShapeDtypeStruct((hslot, levels * pulses), jnp.float32)] * groups
    outs = pl.pallas_call(
        functools.partial(finish_kernel, groups, hslot, pulses, send),
        out_shape=shapes,
        interpret=INTERPRET,
        name="finish_send" if send else "finish",
    )(partial, *incoming, remote_matrix, keep, living, select)
    return outs[0], outs[1:]


def per_device(
    n, concentration, flux_weight, vertical_mixing, deposition, halo_index, send_cells, live_count
):
    levels, pulses, capacity = concentration.shape
    hslot = send_cells.shape[2]
    nbr = flux_weight.shape[0]
    partners = pairings(n)
    groups = len(partners)
    me = lax.axis_index("cells")
    f32 = jnp.float32

    peers = jnp.clip(jnp.stack([partner(me, jnp) for partner in partners]), 0, n - 1)
    picked = send_cells[0][peers].reshape(groups * hslot)
    select = (picked[:, None] == jnp.arange(capacity, dtype=jnp.int32)[None, :]).astype(f32)

    values = concentration
    outgoing = gather_send(values, select, groups, hslot)

    beyond = halo_index - capacity
    sender = beyond // hslot
    place = beyond % hslot
    group = jnp.full(halo_index.shape, -1, dtype=jnp.int32)
    for g, partner in enumerate(partners):
        group = jnp.where(sender == partner(me, jnp), g, group)
    local_col = jnp.where(beyond < 0, halo_index, -1)
    remote_col = jnp.where((beyond >= 0) & (group >= 0), group * hslot + place, -1)
    onehot_local = (local_col[:, None, :] == jnp.arange(capacity)[None, :, None]).astype(f32)
    onehot_remote = (
        remote_col[:, None, :] == jnp.arange(groups * hslot)[None, :, None]
    ).astype(f32)
    local_matrix = sum(flux_weight[k][:, None, :] * onehot_local[k][None] for k in range(nbr))
    remote_matrix = sum(flux_weight[k][:, None, :] * onehot_remote[k][None] for k in range(nbr))
    weight_sum = sum(flux_weight[k] for k in range(nbr))

    living = (jnp.arange(capacity, dtype=jnp.int32) < live_count[0]).astype(f32)[None, :]
    keep = 1.0 - deposition

    for sweep in range(STEPS):
        incoming = [
            lax.ppermute(outgoing[g], "cells", perm=pair_list(n, partner))
            for g, partner in enumerate(partners)
        ]
        partial = local_part(values, local_matrix, weight_sum, vertical_mixing)
        values, outgoing = finish(
            partial, incoming, remote_matrix, keep, living, select, sweep + 1 < STEPS
        )
    return values


def solution(mesh):
    n = mesh.shape["cells"]
    in_specs = (
        P(None, None, "cells"),
        P(None, None, "cells"),
        P(None, "cells"),
        P(None, "cells"),
        P(None, "cells"),
        P("cells", None, None),
        P("cells"),
    )
    out_specs = P(None, None, "cells")

    def body(*args):
        return per_device(n, *args)

    return jax.shard_map(body, mesh=mesh, in_specs=in_specs, out_specs=out_specs, check_vma=False)
```

```python
import functools

import jax
import numpy as np
import jax.numpy as jnp
from jax import lax
from jax.experimental import pallas as pl
from jax.sharding import PartitionSpec as P

STEPS = 2
HIGHEST = lax.Precision.HIGHEST
INTERPRET = False
NT = (((1,), (1,)), ((), ()))
TN = (((0,), (0,)), ((), ()))


def pairings(n):
    half = n // 2
    return (
        lambda d, xp: (d + half) % n,
        lambda d, xp: d ^ 1,
        lambda d, xp: xp.where(d % 2 == 1, d + 1, d - 1),
        lambda d, xp: xp.where(d % 4 < 2, d + 2, d - 2),
        lambda d, xp: xp.where(d % 4 < 2, d - 2, d + 2),
    )


def pair_list(n, partner):
    pairs = []
    for d in range(n):
        p = int(partner(d, np))
        if 0 <= p < n and p != d:
            pairs.append((d, p))
    return pairs


LEVEL_BLOCKS = 3
PULSE_BLOCKS = 2


def level_block(levels):
    return levels // LEVEL_BLOCKS if levels % LEVEL_BLOCKS == 0 else levels


def full_spec(shape):
    return pl.BlockSpec(shape, lambda i: (0,) * len(shape))


def select_kernel(groups, hslot, values_ref, select_ref, *out_refs):
    select = select_ref[...]
    for level in range(values_ref.shape[0]):
        block = lax.dot_general(
            select, values_ref[level], NT, precision=HIGHEST, preferred_element_type=jnp.float32
        )
        for g in range(groups):
            out_refs[g][level] = block[g * hslot : (g + 1) * hslot]


def gather_send(values, select, groups, hslot):
    levels, pulses, capacity = values.shape
    lb = level_block(levels)
    send_spec = pl.BlockSpec((lb, hslot, pulses), lambda i: (i, 0, 0))
    return pl.pallas_call(
        functools.partial(select_kernel, groups, hslot),
        out_shape=[jax.ShapeDtypeStruct((levels, hslot, pulses), jnp.float32)] * groups,
        grid=(levels // lb,),
        in_specs=[pl.BlockSpec((lb, pulses, capacity), lambda i: (i, 0, 0)), full_spec(select.shape)],
        out_specs=[send_spec] * groups,
        interpret=INTERPRET,
        name="gather_send",
    )(values, select)


def local_kernel(values_ref, local_ref, weight_sum_ref, mixing_ref, out_ref):
    levels = values_ref.shape[0]
    for level in range(levels):
        v = values_ref[level]
        x = v - weight_sum_ref[level : level + 1, :] * v
        x = x + jnp.dot(
            v, local_ref[level], precision=HIGHEST, preferred_element_type=jnp.float32
        )
        if level + 1 < levels:
            x = x + mixing_ref[level : level + 1, :] * (values_ref[level + 1] - v)
        if level > 0:
            x = x - mixing_ref[level - 1 : level, :] * (v - values_ref[level - 1])
        out_ref[level] = x


def local_part(values, local_matrix, weight_sum, mixing):
    levels, pulses, capacity = values.shape
    pb = pulses // PULSE_BLOCKS if pulses % (8 * PULSE_BLOCKS) == 0 else pulses
    value_spec = pl.BlockSpec((levels, pb, capacity), lambda i: (0, i, 0))
    return pl.pallas_call(
        local_kernel,
        out_shape=jax.ShapeDtypeStruct(values.shape, jnp.float32),
        grid=(pulses // pb,),
        in_specs=[
            value_spec,
            full_spec(local_matrix.shape),
            full_spec(weight_sum.shape),
            full_spec(mixing.shape),
        ],
        out_specs=value_spec,
        interpret=INTERPRET,
        name="local_part",
    )(values, local_matrix, weight_sum, mixing)


def finish_kernel(groups, hslot, send, *refs):
    partial_ref = refs[0]
    incoming = refs[1 : 1 + groups]
    remote_ref, keep_ref, living_ref, select_ref = refs[1 + groups : 5 + groups]
    out_ref = refs[5 + groups]
    send_refs = refs[6 + groups :]
    living = living_ref[...] > 0.5
    for level in range(partial_ref.shape[0]):
        received = jnp.concatenate([incoming[g][level] for g in range(groups)], axis=0)
        far = lax.dot_general(
            received, remote_ref[level], TN, precision=HIGHEST, preferred_element_type=jnp.float32
        )
        x = (partial_ref[level] + far) * keep_ref[level]
        x = jnp.where(living, x, 0.0)
        out_ref[level] = x
        if send:
            block = lax.dot_general(
                select_ref[...], x, NT, precision=HIGHEST, preferred_element_type=jnp.float32
            )
            for g in range(groups):
                send_refs[g][level] = block[g * hslot : (g + 1) * hslot]


def finish(partial, incoming, remote_matrix, keep, living, select, send):
    levels, pulses, capacity = partial.shape
    groups = len(incoming)
    hslot = incoming[0].shape[1]
    lb = level_block(levels)
    value_spec = pl.BlockSpec((lb, pulses, capacity), lambda i: (i, 0, 0))
    send_spec = pl.BlockSpec((lb, hslot, pulses), lambda i: (i, 0, 0))
    shapes = [jax.ShapeDtypeStruct(partial.shape, jnp.float32)]
    out_specs = [value_spec]
    if send:
        shapes += [jax.ShapeDtypeStruct((levels, hslot, pulses), jnp.float32)] * groups
        out_specs += [send_spec] * groups
    in_specs = (
        [value_spec]
        + [send_spec] * groups
        + [
            pl.BlockSpec((lb,) + remote_matrix.shape[1:], lambda i: (i, 0, 0)),
            pl.BlockSpec((lb,) + keep.shape[1:], lambda i: (i, 0, 0)),
            full_spec(living.shape),
            full_spec(select.shape),
        ]
    )
    outs = pl.pallas_call(
        functools.partial(finish_kernel, groups, hslot, send),
        out_shape=shapes,
        grid=(levels // lb,),
        in_specs=in_specs,
        out_specs=out_specs,
        interpret=INTERPRET,
        name="finish_send" if send else "finish",
    )(partial, *incoming, remote_matrix, keep, living, select)
    return outs[0], outs[1:]


def per_device(
    n, concentration, flux_weight, vertical_mixing, deposition, halo_index, send_cells, live_count
):
    levels, pulses, capacity = concentration.shape
    hslot = send_cells.shape[2]
    nbr = flux_weight.shape[0]
    partners = pairings(n)
    groups = len(partners)
    me = lax.axis_index("cells")
    f32 = jnp.float32

    peers = jnp.clip(jnp.stack([partner(me, jnp) for partner in partners]), 0, n - 1)
    picked = send_cells[0][peers].reshape(groups * hslot)
    select = (picked[:, None] == jnp.arange(capacity, dtype=jnp.int32)[None, :]).astype(f32)

    values = concentration
    outgoing = gather_send(values, select, groups, hslot)

    beyond = halo_index - capacity
    sender = beyond // hslot
    place = beyond % hslot
    group = jnp.full(halo_index.shape, -1, dtype=jnp.int32)
    for g, partner in enumerate(partners):
        group = jnp.where(sender == partner(me, jnp), g, group)
    local_col = jnp.where(beyond < 0, halo_index, -1)
    remote_col = jnp.where((beyond >= 0) & (group >= 0), group * hslot + place, -1)
    onehot_local = (local_col[:, None, :] == jnp.arange(capacity)[None, :, None]).astype(f32)
    onehot_remote = (
        remote_col[:, None, :] == jnp.arange(groups * hslot)[None, :, None]
    ).astype(f32)
    local_matrix = sum(flux_weight[k][:, None, :] * onehot_local[k][None] for k in range(nbr))
    remote_matrix = sum(flux_weight[k][:, None, :] * onehot_remote[k][None] for k in range(nbr))
    weight_sum = sum(flux_weight[k] for k in range(nbr))

    living = (jnp.arange(capacity, dtype=jnp.int32) < live_count[0]).astype(f32)[None, :]
    keep = (1.0 - deposition)[:, None, :]

    for sweep in range(STEPS):
        incoming = [
            lax.ppermute(outgoing[g], "cells", perm=pair_list(n, partner))
            for g, partner in enumerate(partners)
        ]
        partial = local_part(values, local_matrix, weight_sum, vertical_mixing)
        values, outgoing = finish(
            partial, incoming, remote_matrix, keep, living, select, sweep + 1 < STEPS
        )
    return values


def solution(mesh):
    n = mesh.shape["cells"]
    in_specs = (
        P(None, None, "cells"),
        P(None, None, "cells"),
        P(None, "cells"),
        P(None, "cells"),
        P(None, "cells"),
        P("cells", None, None),
        P("cells"),
    )
    out_specs = P(None, None, "cells")

    def body(*args):
        return per_device(n, *args)

    return jax.shard_map(body, mesh=mesh, in_specs=in_specs, out_specs=out_specs, check_vma=False)
```

```python
import functools

import jax
import numpy as np
import jax.numpy as jnp
from jax import lax
from jax.experimental import pallas as pl
from jax.sharding import PartitionSpec as P

STEPS = 2
HIGHEST = lax.Precision.HIGHEST
INTERPRET = False
NT = (((1,), (1,)), ((), ()))
TN = (((0,), (0,)), ((), ()))


def pairings(n):
    half = n // 2
    return (
        lambda d, xp: (d + half) % n,
        lambda d, xp: d ^ 1,
        lambda d, xp: xp.where(d % 2 == 1, d + 1, d - 1),
        lambda d, xp: xp.where(d % 4 < 2, d + 2, d - 2),
        lambda d, xp: xp.where(d % 4 < 2, d - 2, d + 2),
    )


def pair_list(n, partner):
    pairs = []
    for d in range(n):
        p = int(partner(d, np))
        if 0 <= p < n and p != d:
            pairs.append((d, p))
    return pairs


LEVEL_BLOCKS = 3
PULSE_BLOCKS = 2


def level_block(levels):
    return levels // LEVEL_BLOCKS if levels % LEVEL_BLOCKS == 0 else levels


def full_spec(shape):
    return pl.BlockSpec(shape, lambda i: (0,) * len(shape))


def select_kernel(groups, hslot, values_ref, select_ref, *out_refs):
    select = select_ref[...]
    for level in range(values_ref.shape[0]):
        block = lax.dot_general(
            select, values_ref[level], NT, precision=HIGHEST, preferred_element_type=jnp.float32
        )
        for g in range(groups):
            out_refs[g][level] = block[g * hslot : (g + 1) * hslot]


def gather_send(values, select, groups, hslot):
    levels, pulses, capacity = values.shape
    lb = level_block(levels)
    send_spec = pl.BlockSpec((lb, hslot, pulses), lambda i: (i, 0, 0))
    return pl.pallas_call(
        functools.partial(select_kernel, groups, hslot),
        out_shape=[jax.ShapeDtypeStruct((levels, hslot, pulses), jnp.float32)] * groups,
        grid=(levels // lb,),
        in_specs=[pl.BlockSpec((lb, pulses, capacity), lambda i: (i, 0, 0)), full_spec(select.shape)],
        out_specs=[send_spec] * groups,
        interpret=INTERPRET,
        name="gather_send",
    )(values, select)


def local_kernel(values_ref, local_ref, mixing_ref, out_ref):
    levels = values_ref.shape[0]
    for level in range(levels):
        v = values_ref[level]
        x = v + jnp.dot(
            v, local_ref[level], precision=HIGHEST, preferred_element_type=jnp.float32
        )
        if level + 1 < levels:
            x = x + mixing_ref[level : level + 1, :] * (values_ref[level + 1] - v)
        if level > 0:
            x = x - mixing_ref[level - 1 : level, :] * (v - values_ref[level - 1])
        out_ref[level] = x


def local_part(values, matrix, mixing):
    levels, pulses, capacity = values.shape
    pb = pulses // PULSE_BLOCKS if pulses % (8 * PULSE_BLOCKS) == 0 else pulses
    value_spec = pl.BlockSpec((levels, pb, capacity), lambda i: (0, i, 0))
    return pl.pallas_call(
        local_kernel,
        out_shape=jax.ShapeDtypeStruct(values.shape, jnp.float32),
        grid=(pulses // pb,),
        in_specs=[
            value_spec,
            pl.BlockSpec((levels, capacity, capacity), lambda i: (0, 1, 0)),
            full_spec(mixing.shape),
        ],
        out_specs=value_spec,
        interpret=INTERPRET,
        name="local_part",
    )(values, matrix, mixing)


def finish_kernel(groups, hslot, send, *refs):
    partial_ref = refs[0]
    incoming = refs[1 : 1 + groups]
    remote_ref, deposition_ref, count_ref, select_ref = refs[1 + groups : 5 + groups]
    out_ref = refs[5 + groups]
    send_refs = refs[6 + groups :]
    rows = groups * hslot
    lb = partial_ref.shape[0]
    first = pl.program_id(0) * lb
    capacity = partial_ref.shape[2]
    living = lax.broadcasted_iota(jnp.int32, (1, capacity), 1) < count_ref[...]
    for level in range(lb):
        received = jnp.concatenate([incoming[g][level] for g in range(groups)], axis=0)
        far = lax.dot_general(
            received,
            remote_ref[level, :rows, :],
            TN,
            precision=HIGHEST,
            preferred_element_type=jnp.float32,
        )
        keep = 1.0 - deposition_ref[pl.ds(first + level, 1), :]
        x = (partial_ref[level] + far) * keep
        x = jnp.where(living, x, 0.0)
        out_ref[level] = x
        if send:
            block = lax.dot_general(
                select_ref[...], x, NT, precision=HIGHEST, preferred_element_type=jnp.float32
            )
            for g in range(groups):
                send_refs[g][level] = block[g * hslot : (g + 1) * hslot]


def finish(partial, incoming, matrix, deposition, count, select, send):
    levels, pulses, capacity = partial.shape
    groups = len(incoming)
    hslot = incoming[0].shape[1]
    lb = level_block(levels)
    value_spec = pl.BlockSpec((lb, pulses, capacity), lambda i: (i, 0, 0))
    send_spec = pl.BlockSpec((lb, hslot, pulses), lambda i: (i, 0, 0))
    shapes = [jax.ShapeDtypeStruct(partial.shape, jnp.float32)]
    out_specs = [value_spec]
    if send:
        shapes += [jax.ShapeDtypeStruct((levels, hslot, pulses), jnp.float32)] * groups
        out_specs += [send_spec] * groups
    in_specs = (
        [value_spec]
        + [send_spec] * groups
        + [
            pl.BlockSpec((lb, capacity, capacity), lambda i: (i, 0, 0)),
            full_spec(deposition.shape),
            full_spec(count.shape),
            full_spec(select.shape),
        ]
    )
    outs = pl.pallas_call(
        functools.partial(finish_kernel, groups, hslot, send),
        out_shape=shapes,
        grid=(levels // lb,),
        in_specs=in_specs,
        out_specs=out_specs,
        interpret=INTERPRET,
        name="finish_send" if send else "finish",
    )(partial, *incoming, matrix, deposition, count, select)
    return outs[0], outs[1:]


def per_device(
    n, concentration, flux_weight, vertical_mixing, deposition, halo_index, send_cells, live_count
):
    levels, pulses, capacity = concentration.shape
    hslot = send_cells.shape[2]
    nbr = flux_weight.shape[0]
    partners = pairings(n)
    groups = len(partners)
    me = lax.axis_index("cells")
    f32 = jnp.float32

    peers = jnp.stack([partner(me, jnp) for partner in partners])
    is_peer = peers[:, None] == jnp.arange(n, dtype=jnp.int32)[None, :]
    lanes = jnp.arange(capacity, dtype=jnp.int32)
    hit = is_peer[:, :, None, None] & (send_cells[0][None, :, :, None] == lanes)
    select = jnp.sum(hit.astype(f32), axis=1).reshape(groups * hslot, capacity)

    values = concentration
    outgoing = gather_send(values, select, groups, hslot)

    beyond = halo_index - capacity
    sender = beyond // hslot
    place = beyond % hslot
    row = jnp.where(beyond < 0, capacity + halo_index, -1)
    for g, partner in enumerate(partners):
        row = jnp.where((beyond >= 0) & (sender == partner(me, jnp)), g * hslot + place, row)
    slots = jnp.arange(2 * capacity, dtype=jnp.int32)[:, None]
    diagonal = (slots == capacity + lanes[None, :]).astype(f32)
    matrix = sum(
        flux_weight[k][:, None, :] * ((row[k][None, :] == slots).astype(f32) - diagonal)[None]
        for k in range(nbr)
    )
    count = live_count.reshape(1, 1)

    for sweep in range(STEPS):
        incoming = [
            lax.ppermute(outgoing[g], "cells", perm=pair_list(n, partner))
            for g, partner in enumerate(partners)
        ]
        partial = local_part(values, matrix, vertical_mixing)
        values, outgoing = finish(
            partial, incoming, matrix, deposition, count, select, sweep + 1 < STEPS
        )
    return values


def solution(mesh):
    n = mesh.shape["cells"]
    in_specs = (
        P(None, None, "cells"),
        P(None, None, "cells"),
        P(None, "cells"),
        P(None, "cells"),
        P(None, "cells"),
        P("cells", None, None),
        P("cells"),
    )
    out_specs = P(None, None, "cells")

    def body(*args):
        return per_device(n, *args)

    return jax.shard_map(body, mesh=mesh, in_specs=in_specs, out_specs=out_specs, check_vma=False)
```

```python
import functools

import jax
import numpy as np
import jax.numpy as jnp
from jax import lax
from jax.experimental import pallas as pl
from jax.sharding import PartitionSpec as P

STEPS = 2
HIGHEST = lax.Precision.HIGHEST
INTERPRET = False
NT = (((1,), (1,)), ((), ()))
TN = (((0,), (0,)), ((), ()))


def pairings(n):
    half = n // 2
    return (
        lambda d, xp: d ^ 1,
        lambda d, xp: xp.where(d % 4 < 2, d + 2, d - 2),
        lambda d, xp: (d + half) % n,
        lambda d, xp: xp.where(d % 2 == 1, d + 1, d - 1),
        lambda d, xp: xp.where(d % 4 < 2, d - 2, d + 2),
    )


def pair_list(n, partner):
    pairs = []
    for d in range(n):
        p = int(partner(d, np))
        if 0 <= p < n and p != d:
            pairs.append((d, p))
    return pairs


LEVEL_BLOCKS = 3
PULSE_BLOCKS = 2


def level_block(levels):
    return levels // LEVEL_BLOCKS if levels % LEVEL_BLOCKS == 0 else levels


def full_spec(shape):
    return pl.BlockSpec(shape, lambda i: (0,) * len(shape))


def select_kernel(groups, hslot, values_ref, select_ref, *out_refs):
    select = select_ref[...]
    for level in range(values_ref.shape[0]):
        block = lax.dot_general(
            select, values_ref[level], NT, precision=HIGHEST, preferred_element_type=jnp.float32
        )
        for g in range(groups):
            out_refs[g][level] = block[g * hslot : (g + 1) * hslot]


def gather_send(values, select, groups, hslot):
    levels, pulses, capacity = values.shape
    lb = level_block(levels)
    send_spec = pl.BlockSpec((lb, hslot, pulses), lambda i: (i, 0, 0))
    return pl.pallas_call(
        functools.partial(select_kernel, groups, hslot),
        out_shape=[jax.ShapeDtypeStruct((levels, hslot, pulses), jnp.float32)] * groups,
        grid=(levels // lb,),
        in_specs=[pl.BlockSpec((lb, pulses, capacity), lambda i: (i, 0, 0)), full_spec(select.shape)],
        out_specs=[send_spec] * groups,
        interpret=INTERPRET,
        name="gather_send",
    )(values, select)


def local_kernel(values_ref, local_ref, mixing_ref, out_ref):
    levels = values_ref.shape[0]
    for level in range(levels):
        v = values_ref[level]
        x = v + jnp.dot(
            v, local_ref[level], precision=HIGHEST, preferred_element_type=jnp.float32
        )
        if level + 1 < levels:
            x = x + mixing_ref[level : level + 1, :] * (values_ref[level + 1] - v)
        if level > 0:
            x = x - mixing_ref[level - 1 : level, :] * (v - values_ref[level - 1])
        out_ref[level] = x


def local_part(values, matrix, mixing):
    levels, pulses, capacity = values.shape
    pb = pulses // PULSE_BLOCKS if pulses % (8 * PULSE_BLOCKS) == 0 else pulses
    value_spec = pl.BlockSpec((levels, pb, capacity), lambda i: (0, i, 0))
    return pl.pallas_call(
        local_kernel,
        out_shape=jax.ShapeDtypeStruct(values.shape, jnp.float32),
        grid=(pulses // pb,),
        in_specs=[
            value_spec,
            pl.BlockSpec((levels, capacity, capacity), lambda i: (0, 1, 0)),
            full_spec(mixing.shape),
        ],
        out_specs=value_spec,
        interpret=INTERPRET,
        name="local_part",
    )(values, matrix, mixing)


def finish_kernel(groups, hslot, send, *refs):
    partial_ref = refs[0]
    incoming = refs[1 : 1 + groups]
    remote_ref, deposition_ref, count_ref, select_ref = refs[1 + groups : 5 + groups]
    out_ref = refs[5 + groups]
    send_refs = refs[6 + groups :]
    rows = groups * hslot
    lb = partial_ref.shape[0]
    first = pl.program_id(0) * lb
    capacity = partial_ref.shape[2]
    living = lax.broadcasted_iota(jnp.int32, (1, capacity), 1) < count_ref[...]
    for level in range(lb):
        received = jnp.concatenate([incoming[g][level] for g in range(groups)], axis=0)
        far = lax.dot_general(
            received,
            remote_ref[level, :rows, :],
            TN,
            precision=HIGHEST,
            preferred_element_type=jnp.float32,
        )
        keep = 1.0 - deposition_ref[pl.ds(first + level, 1), :]
        x = (partial_ref[level] + far) * keep
        x = jnp.where(living, x, 0.0)
        out_ref[level] = x
        if send:
            block = lax.dot_general(
                select_ref[...], x, NT, precision=HIGHEST, preferred_element_type=jnp.float32
            )
            for g in range(groups):
                send_refs[g][level] = block[g * hslot : (g + 1) * hslot]


def finish(partial, incoming, matrix, deposition, count, select, send):
    levels, pulses, capacity = partial.shape
    groups = len(incoming)
    hslot = incoming[0].shape[1]
    lb = level_block(levels)
    value_spec = pl.BlockSpec((lb, pulses, capacity), lambda i: (i, 0, 0))
    send_spec = pl.BlockSpec((lb, hslot, pulses), lambda i: (i, 0, 0))
    shapes = [jax.ShapeDtypeStruct(partial.shape, jnp.float32)]
    out_specs = [value_spec]
    if send:
        shapes += [jax.ShapeDtypeStruct((levels, hslot, pulses), jnp.float32)] * groups
        out_specs += [send_spec] * groups
    in_specs = (
        [value_spec]
        + [send_spec] * groups
        + [
            pl.BlockSpec((lb, capacity, capacity), lambda i: (i, 0, 0)),
            full_spec(deposition.shape),
            full_spec(count.shape),
            full_spec(select.shape),
        ]
    )
    outs = pl.pallas_call(
        functools.partial(finish_kernel, groups, hslot, send),
        out_shape=shapes,
        grid=(levels // lb,),
        in_specs=in_specs,
        out_specs=out_specs,
        interpret=INTERPRET,
        name="finish_send" if send else "finish",
    )(partial, *incoming, matrix, deposition, count, select)
    return outs[0], outs[1:]


def per_device(
    n, concentration, flux_weight, vertical_mixing, deposition, halo_index, send_cells, live_count
):
    levels, pulses, capacity = concentration.shape
    hslot = send_cells.shape[2]
    nbr = flux_weight.shape[0]
    partners = pairings(n)
    groups = len(partners)
    me = lax.axis_index("cells")
    f32 = jnp.float32

    peers = jnp.stack([partner(me, jnp) for partner in partners])
    is_peer = peers[:, None] == jnp.arange(n, dtype=jnp.int32)[None, :]
    lanes = jnp.arange(capacity, dtype=jnp.int32)
    hit = is_peer[:, :, None, None] & (send_cells[0][None, :, :, None] == lanes)
    select = jnp.sum(hit.astype(f32), axis=1).reshape(groups * hslot, capacity)

    values = concentration
    outgoing = gather_send(values, select, groups, hslot)

    beyond = halo_index - capacity
    sender = beyond // hslot
    place = beyond % hslot
    row = jnp.where(beyond < 0, capacity + halo_index, -1)
    for g, partner in enumerate(partners):
        row = jnp.where((beyond >= 0) & (sender == partner(me, jnp)), g * hslot + place, row)
    slots = jnp.arange(2 * capacity, dtype=jnp.int32)[:, None]
    diagonal = (slots == capacity + lanes[None, :]).astype(f32)
    matrix = sum(
        flux_weight[k][:, None, :] * ((row[k][None, :] == slots).astype(f32) - diagonal)[None]
        for k in range(nbr)
    )
    count = live_count.reshape(1, 1)

    for sweep in range(STEPS):
        incoming = [
            lax.ppermute(outgoing[g], "cells", perm=pair_list(n, partner))
            for g, partner in enumerate(partners)
        ]
        partial = local_part(values, matrix, vertical_mixing)
        values, outgoing = finish(
            partial, incoming, matrix, deposition, count, select, sweep + 1 < STEPS
        )
    return values


def solution(mesh):
    n = mesh.shape["cells"]
    in_specs = (
        P(None, None, "cells"),
        P(None, None, "cells"),
        P(None, "cells"),
        P(None, "cells"),
        P(None, "cells"),
        P("cells", None, None),
        P("cells"),
    )
    out_specs = P(None, None, "cells")

    def body(*args):
        return per_device(n, *args)

    return jax.shard_map(body, mesh=mesh, in_specs=in_specs, out_specs=out_specs, check_vma=False)
```

```python
import functools

import jax
import numpy as np
import jax.numpy as jnp
from jax import lax
from jax.experimental import pallas as pl
from jax.experimental.pallas import tpu as pltpu
from jax.sharding import PartitionSpec as P

STEPS = 2
HIGHEST = lax.Precision.HIGHEST
INTERPRET = False
NT = (((1,), (1,)), ((), ()))
TN = (((0,), (0,)), ((), ()))


def pairings(n):
    half = n // 2
    return (
        lambda d, xp: d ^ 1,
        lambda d, xp: xp.where(d % 4 < 2, d + 2, d - 2),
        lambda d, xp: (d + half) % n,
        lambda d, xp: xp.where(d % 2 == 1, d + 1, d - 1),
        lambda d, xp: xp.where(d % 4 < 2, d - 2, d + 2),
    )


def pair_list(n, partner):
    pairs = []
    for d in range(n):
        p = int(partner(d, np))
        if 0 <= p < n and p != d:
            pairs.append((d, p))
    return pairs


LEVEL_BLOCKS = 3
PULSE_BLOCKS = 2


def level_block(levels):
    return levels // LEVEL_BLOCKS if levels % LEVEL_BLOCKS == 0 else levels


def full_spec(shape):
    return pl.BlockSpec(shape, lambda i: (0,) * len(shape))


def copy_rows(partners, n, hslot, me_ref, cells_ref, flipped_ref, send_refs, level):
    me = me_ref[0]
    capacity = flipped_ref.shape[0]
    for g, partner in enumerate(partners):
        peer = jnp.clip(partner(me, jnp), 0, n - 1)
        for h in range(hslot):
            row = jnp.clip(cells_ref[peer, h], 0, capacity - 1)
            send_refs[g][level, pl.ds(h, 1), :] = flipped_ref[pl.ds(row, 1), :]


def select_kernel(partners, n, hslot, me_ref, cells_ref, values_ref, *refs):
    send_refs, flipped_ref = refs[:-1], refs[-1]
    for level in range(values_ref.shape[0]):
        flipped_ref[...] = values_ref[level].T
        copy_rows(partners, n, hslot, me_ref, cells_ref, flipped_ref, send_refs, level)


def gather_send(values, me, cells, partners, n, hslot):
    levels, pulses, capacity = values.shape
    groups = len(partners)
    lb = level_block(levels)
    send_spec = pl.BlockSpec((lb, hslot, pulses), lambda i: (i, 0, 0))
    smem = pl.BlockSpec(memory_space=pltpu.SMEM)
    return pl.pallas_call(
        functools.partial(select_kernel, partners, n, hslot),
        out_shape=[jax.ShapeDtypeStruct((levels, hslot, pulses), jnp.float32)] * groups,
        grid=(levels // lb,),
        in_specs=[smem, smem, pl.BlockSpec((lb, pulses, capacity), lambda i: (i, 0, 0))],
        out_specs=[send_spec] * groups,
        scratch_shapes=[pltpu.VMEM((capacity, pulses), jnp.float32)],
        interpret=INTERPRET,
        name="gather_send",
    )(me, cells, values)


def local_kernel(values_ref, local_ref, mixing_ref, out_ref):
    levels = values_ref.shape[0]
    for level in range(levels):
        v = values_ref[level]
        x = v + jnp.dot(
            v, local_ref[level], precision=HIGHEST, preferred_element_type=jnp.float32
        )
        if level + 1 < levels:
            x = x + mixing_ref[level : level + 1, :] * (values_ref[level + 1] - v)
        if level > 0:
            x = x - mixing_ref[level - 1 : level, :] * (v - values_ref[level - 1])
        out_ref[level] = x


def local_part(values, matrix, mixing):
    levels, pulses, capacity = values.shape
    pb = pulses // PULSE_BLOCKS if pulses % (8 * PULSE_BLOCKS) == 0 else pulses
    value_spec = pl.BlockSpec((levels, pb, capacity), lambda i: (0, i, 0))
    return pl.pallas_call(
        local_kernel,
        out_shape=jax.ShapeDtypeStruct(values.shape, jnp.float32),
        grid=(pulses // pb,),
        in_specs=[
            value_spec,
            pl.BlockSpec((levels, capacity, capacity), lambda i: (0, 1, 0)),
            full_spec(mixing.shape),
        ],
        out_specs=value_spec,
        interpret=INTERPRET,
        name="local_part",
    )(values, matrix, mixing)


def finish_kernel(partners, n, hslot, send, me_ref, cells_ref, *refs):
    groups = len(partners)
    partial_ref = refs[0]
    incoming = refs[1 : 1 + groups]
    remote_ref, deposition_ref, count_ref = refs[1 + groups : 4 + groups]
    out_ref = refs[4 + groups]
    send_refs = refs[5 + groups : 5 + 2 * groups] if send else ()
    flipped_ref = refs[-1]
    rows = groups * hslot
    lb = partial_ref.shape[0]
    first = pl.program_id(0) * lb
    capacity = partial_ref.shape[2]
    living = lax.broadcasted_iota(jnp.int32, (1, capacity), 1) < count_ref[...]
    for level in range(lb):
        received = jnp.concatenate([incoming[g][level] for g in range(groups)], axis=0)
        far = lax.dot_general(
            received,
            remote_ref[level, :rows, :],
            TN,
            precision=HIGHEST,
            preferred_element_type=jnp.float32,
        )
        keep = 1.0 - deposition_ref[pl.ds(first + level, 1), :]
        x = (partial_ref[level] + far) * keep
        x = jnp.where(living, x, 0.0)
        out_ref[level] = x
        if send:
            flipped_ref[...] = x.T
            copy_rows(partners, n, hslot, me_ref, cells_ref, flipped_ref, send_refs, level)


def finish(partial, incoming, matrix, deposition, count, me, cells, partners, n, send):
    levels, pulses, capacity = partial.shape
    groups = len(incoming)
    hslot = incoming[0].shape[1]
    smem = pl.BlockSpec(memory_space=pltpu.SMEM)
    lb = level_block(levels)
    value_spec = pl.BlockSpec((lb, pulses, capacity), lambda i: (i, 0, 0))
    send_spec = pl.BlockSpec((lb, hslot, pulses), lambda i: (i, 0, 0))
    shapes = [jax.ShapeDtypeStruct(partial.shape, jnp.float32)]
    out_specs = [value_spec]
    if send:
        shapes += [jax.ShapeDtypeStruct((levels, hslot, pulses), jnp.float32)] * groups
        out_specs += [send_spec] * groups
    in_specs = (
        [smem, smem, value_spec]
        + [send_spec] * groups
        + [
            pl.BlockSpec((lb, capacity, capacity), lambda i: (i, 0, 0)),
            full_spec(deposition.shape),
            full_spec(count.shape),
        ]
    )
    outs = pl.pallas_call(
        functools.partial(finish_kernel, partners, n, hslot, send),
        out_shape=shapes,
        grid=(levels // lb,),
        in_specs=in_specs,
        out_specs=out_specs,
        scratch_shapes=[pltpu.VMEM((capacity, pulses), jnp.float32)],
        interpret=INTERPRET,
        name="finish_send" if send else "finish",
    )(me, cells, partial, *incoming, matrix, deposition, count)
    return outs[0], outs[1:]


def per_device(
    n, concentration, flux_weight, vertical_mixing, deposition, halo_index, send_cells, live_count
):
    levels, pulses, capacity = concentration.shape
    hslot = send_cells.shape[2]
    nbr = flux_weight.shape[0]
    partners = pairings(n)
    groups = len(partners)
    me = lax.axis_index("cells")
    f32 = jnp.float32

    me_array = jnp.reshape(me, (1,)).astype(jnp.int32)
    cells = send_cells[0]
    lanes = jnp.arange(capacity, dtype=jnp.int32)

    values = concentration
    outgoing = gather_send(values, me_array, cells, partners, n, hslot)

    beyond = halo_index - capacity
    sender = beyond // hslot
    place = beyond % hslot
    row = jnp.where(beyond < 0, capacity + halo_index, -1)
    for g, partner in enumerate(partners):
        row = jnp.where((beyond >= 0) & (sender == partner(me, jnp)), g * hslot + place, row)
    slots = jnp.arange(2 * capacity, dtype=jnp.int32)[:, None]
    diagonal = (slots == capacity + lanes[None, :]).astype(f32)
    matrix = sum(
        flux_weight[k][:, None, :] * ((row[k][None, :] == slots).astype(f32) - diagonal)[None]
        for k in range(nbr)
    )
    count = live_count.reshape(1, 1)

    for sweep in range(STEPS):
        incoming = [
            lax.ppermute(outgoing[g], "cells", perm=pair_list(n, partner))
            for g, partner in enumerate(partners)
        ]
        partial = local_part(values, matrix, vertical_mixing)
        values, outgoing = finish(
            partial,
            incoming,
            matrix,
            deposition,
            count,
            me_array,
            cells,
            partners,
            n,
            sweep + 1 < STEPS,
        )
    return values


def solution(mesh):
    n = mesh.shape["cells"]
    in_specs = (
        P(None, None, "cells"),
        P(None, None, "cells"),
        P(None, "cells"),
        P(None, "cells"),
        P(None, "cells"),
        P("cells", None, None),
        P("cells"),
    )
    out_specs = P(None, None, "cells")

    def body(*args):
        return per_device(n, *args)

    return jax.shard_map(body, mesh=mesh, in_specs=in_specs, out_specs=out_specs, check_vma=False)
```

```python
import functools

import jax
import numpy as np
import jax.numpy as jnp
from jax import lax
from jax.experimental import pallas as pl
from jax.sharding import PartitionSpec as P

STEPS = 2
HIGHEST = lax.Precision.HIGHEST
INTERPRET = False
NT = (((1,), (1,)), ((), ()))
TN = (((0,), (0,)), ((), ()))


def pairings(n):
    half = n // 2
    return (
        lambda d, xp: d ^ 1,
        lambda d, xp: xp.where(d % 4 < 2, d + 2, d - 2),
        lambda d, xp: (d + half) % n,
        lambda d, xp: xp.where(d % 2 == 1, d + 1, d - 1),
        lambda d, xp: xp.where(d % 4 < 2, d - 2, d + 2),
    )


def pair_list(n, partner):
    pairs = []
    for d in range(n):
        p = int(partner(d, np))
        if 0 <= p < n and p != d:
            pairs.append((d, p))
    return pairs


LEVEL_BLOCKS = 3
PULSE_BLOCKS = 2


def level_block(levels):
    return levels // LEVEL_BLOCKS if levels % LEVEL_BLOCKS == 0 else levels


def full_spec(shape):
    return pl.BlockSpec(shape, lambda i: (0,) * len(shape))


def select_kernel(groups, hslot, values_ref, select_ref, *out_refs):
    select = select_ref[...]
    for level in range(values_ref.shape[0]):
        block = lax.dot_general(
            select, values_ref[level], NT, precision=HIGHEST, preferred_element_type=jnp.float32
        )
        for g in range(groups):
            out_refs[g][level] = block[g * hslot : (g + 1) * hslot]


def gather_send(values, select, groups, hslot):
    levels, pulses, capacity = values.shape
    return pl.pallas_call(
        functools.partial(select_kernel, groups, hslot),
        out_shape=[jax.ShapeDtypeStruct((levels, hslot, pulses), jnp.float32)] * groups,
        interpret=INTERPRET,
        name="gather_send",
    )(values, select)


def local_kernel(values_ref, local_ref, mixing_ref, out_ref):
    levels = values_ref.shape[0]
    for level in range(levels):
        v = values_ref[level]
        x = v + jnp.dot(
            v, local_ref[level], precision=HIGHEST, preferred_element_type=jnp.float32
        )
        if level + 1 < levels:
            x = x + mixing_ref[level : level + 1, :] * (values_ref[level + 1] - v)
        if level > 0:
            x = x - mixing_ref[level - 1 : level, :] * (v - values_ref[level - 1])
        out_ref[level] = x


def local_part(values, matrix, mixing):
    levels, pulses, capacity = values.shape
    pb = pulses // PULSE_BLOCKS if pulses % (8 * PULSE_BLOCKS) == 0 else pulses
    value_spec = pl.BlockSpec((levels, pb, capacity), lambda i: (0, i, 0))
    return pl.pallas_call(
        local_kernel,
        out_shape=jax.ShapeDtypeStruct(values.shape, jnp.float32),
        grid=(pulses // pb,),
        in_specs=[
            value_spec,
            pl.BlockSpec((levels, capacity, capacity), lambda i: (0, 0, 0)),
            full_spec(mixing.shape),
        ],
        out_specs=value_spec,
        interpret=INTERPRET,
        name="local_part",
    )(values, matrix, mixing)


def finish_kernel(groups, hslot, send, *refs):
    partial_ref = refs[0]
    incoming = refs[1 : 1 + groups]
    remote_refs = refs[1 + groups : 1 + 2 * groups]
    deposition_ref, count_ref, select_ref = refs[1 + 2 * groups : 4 + 2 * groups]
    out_ref = refs[4 + 2 * groups]
    send_refs = refs[5 + 2 * groups :]
    lb = partial_ref.shape[0]
    first = 0
    capacity = partial_ref.shape[2]
    living = lax.broadcasted_iota(jnp.int32, (1, capacity), 1) < count_ref[...]
    for level in range(lb):
        received = jnp.concatenate([incoming[g][level] for g in range(groups)], axis=0)
        weights = jnp.concatenate([remote_refs[g][level] for g in range(groups)], axis=0)
        far = lax.dot_general(
            received,
            weights,
            TN,
            precision=HIGHEST,
            preferred_element_type=jnp.float32,
        )
        keep = 1.0 - deposition_ref[first + level : first + level + 1, :]
        x = (partial_ref[level] + far) * keep
        x = jnp.where(living, x, 0.0)
        out_ref[level] = x
        if send:
            block = lax.dot_general(
                select_ref[...], x, NT, precision=HIGHEST, preferred_element_type=jnp.float32
            )
            for g in range(groups):
                send_refs[g][level] = block[g * hslot : (g + 1) * hslot]


def finish(partial, incoming, matrix, deposition, count, select, send):
    levels, pulses, capacity = partial.shape
    groups = len(incoming)
    hslot = incoming[0].shape[1]
    shapes = [jax.ShapeDtypeStruct(partial.shape, jnp.float32)]
    if send:
        shapes += [jax.ShapeDtypeStruct((levels, hslot, pulses), jnp.float32)] * groups
    operands = [partial, *incoming, *([matrix] * groups), deposition, count, select]
    specs = [full_spec(x.shape) for x in operands]
    for g in range(groups):
        block = capacity // hslot + g
        specs[1 + groups + g] = pl.BlockSpec(
            (levels, hslot, capacity), lambda i, block=block: (0, block, 0)
        )
    outs = pl.pallas_call(
        functools.partial(finish_kernel, groups, hslot, send),
        out_shape=shapes,
        grid=(1,),
        in_specs=specs,
        out_specs=[full_spec(x.shape) for x in shapes],
        interpret=INTERPRET,
        name="finish_send" if send else "finish",
    )(*operands)
    return outs[0], outs[1:]


def per_device(
    n, concentration, flux_weight, vertical_mixing, deposition, halo_index, send_cells, live_count
):
    levels, pulses, capacity = concentration.shape
    hslot = send_cells.shape[2]
    nbr = flux_weight.shape[0]
    partners = pairings(n)
    groups = len(partners)
    me = lax.axis_index("cells")
    f32 = jnp.float32

    peers = jnp.stack([partner(me, jnp) for partner in partners])
    is_peer = peers[:, None] == jnp.arange(n, dtype=jnp.int32)[None, :]
    lanes = jnp.arange(capacity, dtype=jnp.int32)
    hit = is_peer[:, :, None, None] & (send_cells[0][None, :, :, None] == lanes)
    select = jnp.sum(hit.astype(f32), axis=1).reshape(groups * hslot, capacity)

    values = concentration
    outgoing = gather_send(values, select, groups, hslot)

    beyond = halo_index - capacity
    sender = beyond // hslot
    place = beyond % hslot
    row = jnp.where(beyond < 0, halo_index, -1)
    for g, partner in enumerate(partners):
        row = jnp.where(
            (beyond >= 0) & (sender == partner(me, jnp)), capacity + g * hslot + place, row
        )
    slots = jnp.arange(capacity + groups * hslot, dtype=jnp.int32)[:, None]
    diagonal = (slots == lanes[None, :]).astype(f32)
    matrix = sum(
        flux_weight[k][:, None, :] * ((row[k][None, :] == slots).astype(f32) - diagonal)[None]
        for k in range(nbr)
    )
    count = live_count.reshape(1, 1)

    for sweep in range(STEPS):
        incoming = [
            lax.ppermute(outgoing[g], "cells", perm=pair_list(n, partner))
            for g, partner in enumerate(partners)
        ]
        partial = local_part(values, matrix, vertical_mixing)
        values, outgoing = finish(
            partial, incoming, matrix, deposition, count, select, sweep + 1 < STEPS
        )
    return values


def solution(mesh):
    n = mesh.shape["cells"]
    in_specs = (
        P(None, None, "cells"),
        P(None, None, "cells"),
        P(None, "cells"),
        P(None, "cells"),
        P(None, "cells"),
        P("cells", None, None),
        P("cells"),
    )
    out_specs = P(None, None, "cells")

    def body(*args):
        return per_device(n, *args)

    return jax.shard_map(body, mesh=mesh, in_specs=in_specs, out_specs=out_specs, check_vma=False)
```

```python
import functools

import jax
import numpy as np
import jax.numpy as jnp
from jax import lax
from jax.experimental import pallas as pl
from jax.sharding import PartitionSpec as P

STEPS = 2
HIGHEST = lax.Precision.HIGHEST
INTERPRET = False
NT = (((1,), (1,)), ((), ()))
TN = (((0,), (0,)), ((), ()))


def pairings(n):
    half = n // 2
    return (
        lambda d, xp: d ^ 1,
        lambda d, xp: xp.where(d % 4 < 2, d + 2, d - 2),
        lambda d, xp: (d + half) % n,
        lambda d, xp: xp.where(d % 2 == 1, d + 1, d - 1),
        lambda d, xp: xp.where(d % 4 < 2, d - 2, d + 2),
    )


def pair_list(n, partner):
    pairs = []
    for d in range(n):
        p = int(partner(d, np))
        if 0 <= p < n and p != d:
            pairs.append((d, p))
    return pairs


LEVEL_BLOCKS = 3
PULSE_BLOCKS = 2


def level_block(levels):
    return levels // LEVEL_BLOCKS if levels % LEVEL_BLOCKS == 0 else levels


def full_spec(shape):
    return pl.BlockSpec(shape, lambda i: (0,) * len(shape))


def select_kernel(groups, hslot, values_ref, select_ref, *out_refs):
    select = select_ref[...]
    for level in range(values_ref.shape[0]):
        block = lax.dot_general(
            select, values_ref[level], NT, precision=HIGHEST, preferred_element_type=jnp.float32
        )
        for g in range(groups):
            out_refs[g][level] = block[g * hslot : (g + 1) * hslot]


def gather_send(values, select, groups, hslot):
    levels, pulses, capacity = values.shape
    return pl.pallas_call(
        functools.partial(select_kernel, groups, hslot),
        out_shape=[jax.ShapeDtypeStruct((levels, hslot, pulses), jnp.float32)] * groups,
        interpret=INTERPRET,
        name="gather_send",
    )(values, select)


def local_kernel(values_ref, local_ref, mixing_ref, out_ref):
    levels = values_ref.shape[0]
    for level in range(levels):
        v = values_ref[level]
        x = v + jnp.dot(
            v, local_ref[level], precision=HIGHEST, preferred_element_type=jnp.float32
        )
        if level + 1 < levels:
            x = x + mixing_ref[level : level + 1, :] * (values_ref[level + 1] - v)
        if level > 0:
            x = x - mixing_ref[level - 1 : level, :] * (v - values_ref[level - 1])
        out_ref[level] = x


def local_part(values, matrix, mixing):
    levels, pulses, capacity = values.shape
    pb = pulses // PULSE_BLOCKS if pulses % (8 * PULSE_BLOCKS) == 0 else pulses
    value_spec = pl.BlockSpec((levels, pb, capacity), lambda i: (0, i, 0))
    return pl.pallas_call(
        local_kernel,
        out_shape=jax.ShapeDtypeStruct(values.shape, jnp.float32),
        grid=(pulses // pb,),
        in_specs=[
            value_spec,
            pl.BlockSpec((levels, capacity, capacity), lambda i: (0, 0, 0)),
            full_spec(mixing.shape),
        ],
        out_specs=value_spec,
        interpret=INTERPRET,
        name="local_part",
    )(values, matrix, mixing)


def finish_kernel(groups, hslot, send, *refs):
    partial_ref = refs[0]
    incoming = refs[1 : 1 + groups]
    remote_refs = refs[1 + groups : 1 + 2 * groups]
    deposition_ref, count_ref, select_ref = refs[1 + 2 * groups : 4 + 2 * groups]
    out_ref = refs[4 + 2 * groups]
    send_refs = refs[5 + 2 * groups :]
    lb = partial_ref.shape[0]
    first = 0
    capacity = partial_ref.shape[2]
    living = lax.broadcasted_iota(jnp.int32, (1, capacity), 1) < count_ref[...]
    for level in range(lb):
        received = jnp.concatenate([incoming[g][level] for g in range(groups)], axis=0)
        weights = jnp.concatenate([remote_refs[g][level] for g in range(groups)], axis=0)
        far = lax.dot_general(
            received,
            weights,
            TN,
            precision=HIGHEST,
            preferred_element_type=jnp.float32,
        )
        keep = 1.0 - deposition_ref[first + level : first + level + 1, :]
        x = (partial_ref[level] + far) * keep
        x = jnp.where(living, x, 0.0)
        out_ref[level] = x
        if send:
            block = lax.dot_general(
                select_ref[...], x, NT, precision=HIGHEST, preferred_element_type=jnp.float32
            )
            for g in range(groups):
                send_refs[g][level] = block[g * hslot : (g + 1) * hslot]


def finish(partial, incoming, matrix, deposition, count, select, send):
    levels, pulses, capacity = partial.shape
    groups = len(incoming)
    hslot = incoming[0].shape[1]
    shapes = [jax.ShapeDtypeStruct(partial.shape, jnp.float32)]
    if send:
        shapes += [jax.ShapeDtypeStruct((levels, hslot, pulses), jnp.float32)] * groups
    operands = [partial, *incoming, *([matrix] * groups), deposition, count, select]
    specs = [full_spec(x.shape) for x in operands]
    for g in range(groups):
        block = capacity // hslot + g
        specs[1 + groups + g] = pl.BlockSpec(
            (levels, hslot, capacity), lambda i, block=block: (0, block, 0)
        )
    outs = pl.pallas_call(
        functools.partial(finish_kernel, groups, hslot, send),
        out_shape=shapes,
        grid=(1,),
        in_specs=specs,
        out_specs=[full_spec(x.shape) for x in shapes],
        interpret=INTERPRET,
        name="finish_send" if send else "finish",
    )(*operands)
    return outs[0], outs[1:]


def per_device(
    n, concentration, flux_weight, vertical_mixing, deposition, halo_index, send_cells, live_count
):
    levels, pulses, capacity = concentration.shape
    hslot = send_cells.shape[2]
    nbr = flux_weight.shape[0]
    partners = pairings(n)
    groups = len(partners)
    me = lax.axis_index("cells")
    f32 = jnp.float32

    peers = jnp.stack([partner(me, jnp) for partner in partners])
    is_peer = peers[:, None] == jnp.arange(n, dtype=jnp.int32)[None, :]
    lanes = jnp.arange(capacity, dtype=jnp.int32)
    slots_by_peer = send_cells[0].T
    hit = is_peer[:, None, :, None] & (slots_by_peer[None, :, :, None] == lanes)
    select = jnp.sum(hit.astype(f32), axis=2).reshape(groups * hslot, capacity)

    values = concentration
    outgoing = gather_send(values, select, groups, hslot)

    beyond = halo_index - capacity
    sender = beyond // hslot
    place = beyond % hslot
    row = jnp.where(beyond < 0, halo_index, -1)
    for g, partner in enumerate(partners):
        row = jnp.where(
            (beyond >= 0) & (sender == partner(me, jnp)), capacity + g * hslot + place, row
        )
    slots = jnp.arange(capacity + groups * hslot, dtype=jnp.int32)[:, None]
    diagonal = (slots == lanes[None, :]).astype(f32)
    matrix = sum(
        flux_weight[k][:, None, :] * ((row[k][None, :] == slots).astype(f32) - diagonal)[None]
        for k in range(nbr)
    )
    count = live_count.reshape(1, 1)

    for sweep in range(STEPS):
        incoming = [
            lax.ppermute(outgoing[g], "cells", perm=pair_list(n, partner))
            for g, partner in enumerate(partners)
        ]
        partial = local_part(values, matrix, vertical_mixing)
        values, outgoing = finish(
            partial, incoming, matrix, deposition, count, select, sweep + 1 < STEPS
        )
    return values


def solution(mesh):
    n = mesh.shape["cells"]
    in_specs = (
        P(None, None, "cells"),
        P(None, None, "cells"),
        P(None, "cells"),
        P(None, "cells"),
        P(None, "cells"),
        P("cells", None, None),
        P("cells"),
    )
    out_specs = P(None, None, "cells")

    def body(*args):
        return per_device(n, *args)

    return jax.shard_map(body, mesh=mesh, in_specs=in_specs, out_specs=out_specs, check_vma=False)
```

```python
import functools

import jax
import numpy as np
import jax.numpy as jnp
from jax import lax
from jax.experimental import pallas as pl
from jax.sharding import PartitionSpec as P

STEPS = 2
HIGHEST = lax.Precision.HIGHEST
INTERPRET = False
NT = (((1,), (1,)), ((), ()))
TN = (((0,), (0,)), ((), ()))


def pairings(n):
    half = n // 2
    return (
        lambda d, xp: d ^ 1,
        lambda d, xp: xp.where(d % 4 < 2, d + 2, d - 2),
        lambda d, xp: xp.where(d % 2 == 1, d + 1, d - 1),
        lambda d, xp: xp.where(d % 4 < 2, d - 2, d + 2),
        lambda d, xp: (d + half) % n,
    )


def pair_list(n, partner):
    pairs = []
    for d in range(n):
        p = int(partner(d, np))
        if 0 <= p < n and p != d:
            pairs.append((d, p))
    return pairs


LEVEL_BLOCKS = 3
PULSE_BLOCKS = 2


def level_block(levels):
    return levels // LEVEL_BLOCKS if levels % LEVEL_BLOCKS == 0 else levels


def full_spec(shape):
    return pl.BlockSpec(shape, lambda i: (0,) * len(shape))


def select_kernel(groups, hslot, values_ref, select_ref, *out_refs):
    select = select_ref[...]
    for level in range(values_ref.shape[0]):
        block = lax.dot_general(
            select, values_ref[level], NT, precision=HIGHEST, preferred_element_type=jnp.float32
        )
        for g in range(groups):
            out_refs[g][level] = block[g * hslot : (g + 1) * hslot]


def gather_send(values, select, groups, hslot):
    levels, pulses, capacity = values.shape
    return pl.pallas_call(
        functools.partial(select_kernel, groups, hslot),
        out_shape=[jax.ShapeDtypeStruct((levels, hslot, pulses), jnp.float32)] * groups,
        interpret=INTERPRET,
        name="gather_send",
    )(values, select)


def local_kernel(values_ref, local_ref, mixing_ref, out_ref):
    levels = values_ref.shape[0]
    for level in range(levels):
        v = values_ref[level]
        x = v + jnp.dot(
            v, local_ref[level], precision=HIGHEST, preferred_element_type=jnp.float32
        )
        if level + 1 < levels:
            x = x + mixing_ref[level : level + 1, :] * (values_ref[level + 1] - v)
        if level > 0:
            x = x - mixing_ref[level - 1 : level, :] * (v - values_ref[level - 1])
        out_ref[level] = x


def local_part(values, matrix, mixing):
    levels, pulses, capacity = values.shape
    pb = pulses // PULSE_BLOCKS if pulses % (8 * PULSE_BLOCKS) == 0 else pulses
    value_spec = pl.BlockSpec((levels, pb, capacity), lambda i: (0, i, 0))
    return pl.pallas_call(
        local_kernel,
        out_shape=jax.ShapeDtypeStruct(values.shape, jnp.float32),
        grid=(pulses // pb,),
        in_specs=[
            value_spec,
            pl.BlockSpec((levels, capacity, capacity), lambda i: (0, 0, 0)),
            full_spec(mixing.shape),
        ],
        out_specs=value_spec,
        interpret=INTERPRET,
        name="local_part",
    )(values, matrix, mixing)


def finish_kernel(groups, hslot, send, *refs):
    partial_ref = refs[0]
    incoming = refs[1 : 1 + groups]
    remote_refs = refs[1 + groups : 1 + 2 * groups]
    deposition_ref, count_ref, select_ref = refs[1 + 2 * groups : 4 + 2 * groups]
    out_ref = refs[4 + 2 * groups]
    send_refs = refs[5 + 2 * groups :]
    lb = partial_ref.shape[0]
    first = 0
    capacity = partial_ref.shape[2]
    living = lax.broadcasted_iota(jnp.int32, (1, capacity), 1) < count_ref[...]
    for level in range(lb):
        received = jnp.concatenate([incoming[g][level] for g in range(groups)], axis=0)
        weights = jnp.concatenate([remote_refs[g][level] for g in range(groups)], axis=0)
        far = lax.dot_general(
            received,
            weights,
            TN,
            precision=HIGHEST,
            preferred_element_type=jnp.float32,
        )
        keep = 1.0 - deposition_ref[first + level : first + level + 1, :]
        x = (partial_ref[level] + far) * keep
        x = jnp.where(living, x, 0.0)
        out_ref[level] = x
        if send:
            block = lax.dot_general(
                select_ref[...], x, NT, precision=HIGHEST, preferred_element_type=jnp.float32
            )
            for g in range(groups):
                send_refs[g][level] = block[g * hslot : (g + 1) * hslot]


def finish(partial, incoming, matrix, deposition, count, select, send):
    levels, pulses, capacity = partial.shape
    groups = len(incoming)
    hslot = incoming[0].shape[1]
    shapes = [jax.ShapeDtypeStruct(partial.shape, jnp.float32)]
    if send:
        shapes += [jax.ShapeDtypeStruct((levels, hslot, pulses), jnp.float32)] * groups
    operands = [partial, *incoming, *([matrix] * groups), deposition, count, select]
    specs = [full_spec(x.shape) for x in operands]
    for g in range(groups):
        block = capacity // hslot + g
        specs[1 + groups + g] = pl.BlockSpec(
            (levels, hslot, capacity), lambda i, block=block: (0, block, 0)
        )
    outs = pl.pallas_call(
        functools.partial(finish_kernel, groups, hslot, send),
        out_shape=shapes,
        grid=(1,),
        in_specs=specs,
        out_specs=[full_spec(x.shape) for x in shapes],
        interpret=INTERPRET,
        name="finish_send" if send else "finish",
    )(*operands)
    return outs[0], outs[1:]


def per_device(
    n, concentration, flux_weight, vertical_mixing, deposition, halo_index, send_cells, live_count
):
    levels, pulses, capacity = concentration.shape
    hslot = send_cells.shape[2]
    nbr = flux_weight.shape[0]
    partners = pairings(n)
    groups = len(partners)
    me = lax.axis_index("cells")
    f32 = jnp.float32

    peers = jnp.stack([partner(me, jnp) for partner in partners])
    is_peer = peers[:, None] == jnp.arange(n, dtype=jnp.int32)[None, :]
    lanes = jnp.arange(capacity, dtype=jnp.int32)
    slots_by_peer = send_cells[0].T
    hit = is_peer[:, None, :, None] & (slots_by_peer[None, :, :, None] == lanes)
    select = jnp.sum(hit.astype(f32), axis=2).reshape(groups * hslot, capacity)

    values = concentration
    outgoing = gather_send(values, select, groups, hslot)

    beyond = halo_index - capacity
    sender = beyond // hslot
    place = beyond % hslot
    row = jnp.where(beyond < 0, halo_index, -1)
    for g, partner in enumerate(partners):
        row = jnp.where(
            (beyond >= 0) & (sender == partner(me, jnp)), capacity + g * hslot + place, row
        )
    slots = jnp.arange(capacity + groups * hslot, dtype=jnp.int32)[:, None]
    diagonal = (slots == lanes[None, :]).astype(f32)
    matrix = sum(
        flux_weight[k][:, None, :] * ((row[k][None, :] == slots).astype(f32) - diagonal)[None]
        for k in range(nbr)
    )
    count = live_count.reshape(1, 1)

    for sweep in range(STEPS):
        incoming = [
            lax.ppermute(outgoing[g], "cells", perm=pair_list(n, partner))
            for g, partner in enumerate(partners)
        ]
        partial = local_part(values, matrix, vertical_mixing)
        values, outgoing = finish(
            partial, incoming, matrix, deposition, count, select, sweep + 1 < STEPS
        )
    return values


def solution(mesh):
    n = mesh.shape["cells"]
    in_specs = (
        P(None, None, "cells"),
        P(None, None, "cells"),
        P(None, "cells"),
        P(None, "cells"),
        P(None, "cells"),
        P("cells", None, None),
        P("cells"),
    )
    out_specs = P(None, None, "cells")

    def body(*args):
        return per_device(n, *args)

    return jax.shard_map(body, mesh=mesh, in_specs=in_specs, out_specs=out_specs, check_vma=False)
```

```python
import functools

import jax
import numpy as np
import jax.numpy as jnp
from jax import lax
from jax.experimental import pallas as pl
from jax.sharding import PartitionSpec as P

STEPS = 2
HIGHEST = lax.Precision.HIGHEST
INTERPRET = False
NT = (((1,), (1,)), ((), ()))
TN = (((0,), (0,)), ((), ()))


def pairings(n):
    half = n // 2
    return (
        lambda d, xp: d ^ 1,
        lambda d, xp: (d + half) % n,
        lambda d, xp: xp.where(d % 4 < 2, d + 2, d - 2),
        lambda d, xp: xp.where(d % 2 == 1, d + 1, d - 1),
        lambda d, xp: xp.where(d % 4 < 2, d - 2, d + 2),
    )


def pair_list(n, partner):
    pairs = []
    for d in range(n):
        p = int(partner(d, np))
        if 0 <= p < n and p != d:
            pairs.append((d, p))
    return pairs


LEVEL_BLOCKS = 3
PULSE_BLOCKS = 2


def level_block(levels):
    return levels // LEVEL_BLOCKS if levels % LEVEL_BLOCKS == 0 else levels


def full_spec(shape):
    return pl.BlockSpec(shape, lambda i: (0,) * len(shape))


def select_kernel(groups, hslot, values_ref, select_ref, *out_refs):
    select = select_ref[...]
    for level in range(values_ref.shape[0]):
        block = lax.dot_general(
            select, values_ref[level], NT, precision=HIGHEST, preferred_element_type=jnp.float32
        )
        for g in range(groups):
            out_refs[g][level] = block[g * hslot : (g + 1) * hslot]


def gather_send(values, select, groups, hslot):
    levels, pulses, capacity = values.shape
    return pl.pallas_call(
        functools.partial(select_kernel, groups, hslot),
        out_shape=[jax.ShapeDtypeStruct((levels, hslot, pulses), jnp.float32)] * groups,
        interpret=INTERPRET,
        name="gather_send",
    )(values, select)


def local_kernel(values_ref, local_ref, mixing_ref, out_ref):
    levels = values_ref.shape[0]
    for level in range(levels):
        v = values_ref[level]
        x = v + jnp.dot(
            v, local_ref[level], precision=HIGHEST, preferred_element_type=jnp.float32
        )
        if level + 1 < levels:
            x = x + mixing_ref[level : level + 1, :] * (values_ref[level + 1] - v)
        if level > 0:
            x = x - mixing_ref[level - 1 : level, :] * (v - values_ref[level - 1])
        out_ref[level] = x


def local_part(values, matrix, mixing):
    levels, pulses, capacity = values.shape
    pb = pulses // PULSE_BLOCKS if pulses % (8 * PULSE_BLOCKS) == 0 else pulses
    value_spec = pl.BlockSpec((levels, pb, capacity), lambda i: (0, i, 0))
    return pl.pallas_call(
        local_kernel,
        out_shape=jax.ShapeDtypeStruct(values.shape, jnp.float32),
        grid=(pulses // pb,),
        in_specs=[
            value_spec,
            pl.BlockSpec((levels, capacity, capacity), lambda i: (0, 0, 0)),
            full_spec(mixing.shape),
        ],
        out_specs=value_spec,
        interpret=INTERPRET,
        name="local_part",
    )(values, matrix, mixing)


def finish_kernel(groups, hslot, send, *refs):
    partial_ref = refs[0]
    incoming = refs[1 : 1 + groups]
    remote_refs = refs[1 + groups : 1 + 2 * groups]
    deposition_ref, count_ref, select_ref = refs[1 + 2 * groups : 4 + 2 * groups]
    out_ref = refs[4 + 2 * groups]
    send_refs = refs[5 + 2 * groups :]
    lb = partial_ref.shape[0]
    first = 0
    capacity = partial_ref.shape[2]
    living = lax.broadcasted_iota(jnp.int32, (1, capacity), 1) < count_ref[...]
    for level in range(lb):
        received = jnp.concatenate([incoming[g][level] for g in range(groups)], axis=0)
        weights = jnp.concatenate([remote_refs[g][level] for g in range(groups)], axis=0)
        far = lax.dot_general(
            received,
            weights,
            TN,
            precision=HIGHEST,
            preferred_element_type=jnp.float32,
        )
        keep = 1.0 - deposition_ref[first + level : first + level + 1, :]
        x = (partial_ref[level] + far) * keep
        x = jnp.where(living, x, 0.0)
        out_ref[level] = x
        if send:
            block = lax.dot_general(
                select_ref[...], x, NT, precision=HIGHEST, preferred_element_type=jnp.float32
            )
            for g in range(groups):
                send_refs[g][level] = block[g * hslot : (g + 1) * hslot]


def finish(partial, incoming, matrix, deposition, count, select, send):
    levels, pulses, capacity = partial.shape
    groups = len(incoming)
    hslot = incoming[0].shape[1]
    shapes = [jax.ShapeDtypeStruct(partial.shape, jnp.float32)]
    if send:
        shapes += [jax.ShapeDtypeStruct((levels, hslot, pulses), jnp.float32)] * groups
    operands = [partial, *incoming, *([matrix] * groups), deposition, count, select]
    specs = [full_spec(x.shape) for x in operands]
    for g in range(groups):
        block = capacity // hslot + g
        specs[1 + groups + g] = pl.BlockSpec(
            (levels, hslot, capacity), lambda i, block=block: (0, block, 0)
        )
    outs = pl.pallas_call(
        functools.partial(finish_kernel, groups, hslot, send),
        out_shape=shapes,
        grid=(1,),
        in_specs=specs,
        out_specs=[full_spec(x.shape) for x in shapes],
        interpret=INTERPRET,
        name="finish_send" if send else "finish",
    )(*operands)
    return outs[0], outs[1:]


def per_device(
    n, concentration, flux_weight, vertical_mixing, deposition, halo_index, send_cells, live_count
):
    levels, pulses, capacity = concentration.shape
    hslot = send_cells.shape[2]
    nbr = flux_weight.shape[0]
    partners = pairings(n)
    groups = len(partners)
    me = lax.axis_index("cells")
    f32 = jnp.float32

    peers = jnp.stack([partner(me, jnp) for partner in partners])
    is_peer = peers[:, None] == jnp.arange(n, dtype=jnp.int32)[None, :]
    lanes = jnp.arange(capacity, dtype=jnp.int32)
    slots_by_peer = send_cells[0].T
    hit = is_peer[:, None, :, None] & (slots_by_peer[None, :, :, None] == lanes)
    select = jnp.sum(hit.astype(f32), axis=2).reshape(groups * hslot, capacity)

    values = concentration
    outgoing = gather_send(values, select, groups, hslot)

    beyond = halo_index - capacity
    sender = beyond // hslot
    place = beyond % hslot
    row = jnp.where(beyond < 0, halo_index, -1)
    for g, partner in enumerate(partners):
        row = jnp.where(
            (beyond >= 0) & (sender == partner(me, jnp)), capacity + g * hslot + place, row
        )
    slots = jnp.arange(capacity + groups * hslot, dtype=jnp.int32)[:, None]
    diagonal = (slots == lanes[None, :]).astype(f32)
    matrix = sum(
        flux_weight[k][:, None, :] * ((row[k][None, :] == slots).astype(f32) - diagonal)[None]
        for k in range(nbr)
    )
    count = live_count.reshape(1, 1)

    for sweep in range(STEPS):
        incoming = [
            lax.ppermute(outgoing[g], "cells", perm=pair_list(n, partner))
            for g, partner in enumerate(partners)
        ]
        partial = local_part(values, matrix, vertical_mixing)
        values, outgoing = finish(
            partial, incoming, matrix, deposition, count, select, sweep + 1 < STEPS
        )
    return values


def solution(mesh):
    n = mesh.shape["cells"]
    in_specs = (
        P(None, None, "cells"),
        P(None, None, "cells"),
        P(None, "cells"),
        P(None, "cells"),
        P(None, "cells"),
        P("cells", None, None),
        P("cells"),
    )
    out_specs = P(None, None, "cells")

    def body(*args):
        return per_device(n, *args)

    return jax.shard_map(body, mesh=mesh, in_specs=in_specs, out_specs=out_specs, check_vma=False)
```

```python
import functools

import jax
import numpy as np
import jax.numpy as jnp
from jax import lax
from jax.experimental import pallas as pl
from jax.sharding import PartitionSpec as P

STEPS = 2
HIGHEST = lax.Precision.HIGHEST
INTERPRET = False
NT = (((1,), (1,)), ((), ()))
TN = (((0,), (0,)), ((), ()))


def pairings(n):
    half = n // 2
    return (
        lambda d, xp: d ^ 1,
        lambda d, xp: xp.where(d % 4 < 2, d + 2, d - 2),
        lambda d, xp: (d + half) % n,
        lambda d, xp: xp.where(d % 2 == 1, d + 1, d - 1),
        lambda d, xp: xp.where(d % 4 < 2, d - 2, d + 2),
    )


def pair_list(n, partner):
    pairs = []
    for d in range(n):
        p = int(partner(d, np))
        if 0 <= p < n and p != d:
            pairs.append((d, p))
    return pairs


LEVEL_BLOCKS = 3
PULSE_BLOCKS = 2


def level_block(levels):
    return levels // LEVEL_BLOCKS if levels % LEVEL_BLOCKS == 0 else levels


def full_spec(shape):
    return pl.BlockSpec(shape, lambda i: (0,) * len(shape))


def select_kernel(partners, hslot, slots_ref, values_ref, *refs):
    groups = len(partners)
    out_refs, select_ref = refs[:groups], refs[groups]
    me = lax.axis_index("cells")
    capacity = values_ref.shape[2]
    slots = slots_ref[...].astype(jnp.float32)
    peer_index = lax.broadcasted_iota(jnp.int32, slots.shape, 1)
    lanes = lax.broadcasted_iota(jnp.int32, (hslot, capacity), 1).astype(jnp.float32)
    for g, partner in enumerate(partners):
        peer = partner(me, jnp)
        column = jnp.sum(jnp.where(peer_index == peer, slots, 0.0), axis=1, keepdims=True)
        select_ref[g * hslot : (g + 1) * hslot, :] = (lanes == column).astype(jnp.float32)
    select = select_ref[...]
    for level in range(values_ref.shape[0]):
        block = lax.dot_general(
            select, values_ref[level], NT, precision=HIGHEST, preferred_element_type=jnp.float32
        )
        for g in range(groups):
            out_refs[g][level] = block[g * hslot : (g + 1) * hslot]


def gather_send(values, slots, partners, hslot):
    levels, pulses, capacity = values.shape
    groups = len(partners)
    shapes = [jax.ShapeDtypeStruct((levels, hslot, pulses), jnp.float32)] * groups
    shapes.append(jax.ShapeDtypeStruct((groups * hslot, capacity), jnp.float32))
    outs = pl.pallas_call(
        functools.partial(select_kernel, partners, hslot),
        out_shape=shapes,
        interpret=INTERPRET,
        name="gather_send",
    )(slots, values)
    return outs[:groups], outs[groups]


def local_kernel(values_ref, local_ref, mixing_ref, out_ref):
    levels = values_ref.shape[0]
    for level in range(levels):
        v = values_ref[level]
        x = v + jnp.dot(
            v, local_ref[level], precision=HIGHEST, preferred_element_type=jnp.float32
        )
        if level + 1 < levels:
            x = x + mixing_ref[level : level + 1, :] * (values_ref[level + 1] - v)
        if level > 0:
            x = x - mixing_ref[level - 1 : level, :] * (v - values_ref[level - 1])
        out_ref[level] = x


def local_part(values, matrix, mixing):
    levels, pulses, capacity = values.shape
    pb = pulses // PULSE_BLOCKS if pulses % (8 * PULSE_BLOCKS) == 0 else pulses
    value_spec = pl.BlockSpec((levels, pb, capacity), lambda i: (0, i, 0))
    return pl.pallas_call(
        local_kernel,
        out_shape=jax.ShapeDtypeStruct(values.shape, jnp.float32),
        grid=(pulses // pb,),
        in_specs=[
            value_spec,
            pl.BlockSpec((levels, capacity, capacity), lambda i: (0, 0, 0)),
            full_spec(mixing.shape),
        ],
        out_specs=value_spec,
        interpret=INTERPRET,
        name="local_part",
    )(values, matrix, mixing)


def finish_kernel(groups, hslot, send, *refs):
    partial_ref = refs[0]
    incoming = refs[1 : 1 + groups]
    remote_refs = refs[1 + groups : 1 + 2 * groups]
    deposition_ref, count_ref, select_ref = refs[1 + 2 * groups : 4 + 2 * groups]
    out_ref = refs[4 + 2 * groups]
    send_refs = refs[5 + 2 * groups :]
    lb = partial_ref.shape[0]
    first = 0
    capacity = partial_ref.shape[2]
    living = lax.broadcasted_iota(jnp.int32, (1, capacity), 1) < count_ref[...]
    for level in range(lb):
        received = jnp.concatenate([incoming[g][level] for g in range(groups)], axis=0)
        weights = jnp.concatenate([remote_refs[g][level] for g in range(groups)], axis=0)
        far = lax.dot_general(
            received,
            weights,
            TN,
            precision=HIGHEST,
            preferred_element_type=jnp.float32,
        )
        keep = 1.0 - deposition_ref[first + level : first + level + 1, :]
        x = (partial_ref[level] + far) * keep
        x = jnp.where(living, x, 0.0)
        out_ref[level] = x
        if send:
            block = lax.dot_general(
                select_ref[...], x, NT, precision=HIGHEST, preferred_element_type=jnp.float32
            )
            for g in range(groups):
                send_refs[g][level] = block[g * hslot : (g + 1) * hslot]


def finish(partial, incoming, matrix, deposition, count, select, send):
    levels, pulses, capacity = partial.shape
    groups = len(incoming)
    hslot = incoming[0].shape[1]
    shapes = [jax.ShapeDtypeStruct(partial.shape, jnp.float32)]
    if send:
        shapes += [jax.ShapeDtypeStruct((levels, hslot, pulses), jnp.float32)] * groups
    operands = [partial, *incoming, *([matrix] * groups), deposition, count, select]
    specs = [full_spec(x.shape) for x in operands]
    for g in range(groups):
        block = capacity // hslot + g
        specs[1 + groups + g] = pl.BlockSpec(
            (levels, hslot, capacity), lambda i, block=block: (0, block, 0)
        )
    outs = pl.pallas_call(
        functools.partial(finish_kernel, groups, hslot, send),
        out_shape=shapes,
        grid=(1,),
        in_specs=specs,
        out_specs=[full_spec(x.shape) for x in shapes],
        interpret=INTERPRET,
        name="finish_send" if send else "finish",
    )(*operands)
    return outs[0], outs[1:]


def per_device(
    n, concentration, flux_weight, vertical_mixing, deposition, halo_index, send_cells, live_count
):
    levels, pulses, capacity = concentration.shape
    hslot = send_cells.shape[2]
    nbr = flux_weight.shape[0]
    partners = pairings(n)
    groups = len(partners)
    me = lax.axis_index("cells")
    f32 = jnp.float32

    lanes = jnp.arange(capacity, dtype=jnp.int32)
    values = concentration
    outgoing, select = gather_send(values, send_cells[0].T, partners, hslot)

    beyond = halo_index - capacity
    sender = beyond // hslot
    place = beyond % hslot
    row = jnp.where(beyond < 0, halo_index, -1)
    for g, partner in enumerate(partners):
        row = jnp.where(
            (beyond >= 0) & (sender == partner(me, jnp)), capacity + g * hslot + place, row
        )
    slots = jnp.arange(capacity + groups * hslot, dtype=jnp.int32)[:, None]
    diagonal = (slots == lanes[None, :]).astype(f32)
    matrix = sum(
        flux_weight[k][:, None, :] * ((row[k][None, :] == slots).astype(f32) - diagonal)[None]
        for k in range(nbr)
    )
    count = live_count.reshape(1, 1)

    for sweep in range(STEPS):
        incoming = [
            lax.ppermute(outgoing[g], "cells", perm=pair_list(n, partner))
            for g, partner in enumerate(partners)
        ]
        partial = local_part(values, matrix, vertical_mixing)
        values, outgoing = finish(
            partial, incoming, matrix, deposition, count, select, sweep + 1 < STEPS
        )
    return values


def solution(mesh):
    n = mesh.shape["cells"]
    in_specs = (
        P(None, None, "cells"),
        P(None, None, "cells"),
        P(None, "cells"),
        P(None, "cells"),
        P(None, "cells"),
        P("cells", None, None),
        P("cells"),
    )
    out_specs = P(None, None, "cells")

    def body(*args):
        return per_device(n, *args)

    return jax.shard_map(body, mesh=mesh, in_specs=in_specs, out_specs=out_specs, check_vma=False)
```

```python
import functools

import jax
import numpy as np
import jax.numpy as jnp
from jax import lax
from jax.experimental import pallas as pl
from jax.experimental.pallas import tpu as pltpu
from jax.sharding import PartitionSpec as P

STEPS = 2
HIGHEST = lax.Precision.HIGHEST
INTERPRET = False
NT = (((1,), (1,)), ((), ()))
TN = (((0,), (0,)), ((), ()))


def pairings(n):
    half = n // 2
    return (
        lambda d, xp: d ^ 1,
        lambda d, xp: xp.where(d % 4 < 2, d + 2, d - 2),
        lambda d, xp: (d + half) % n,
        lambda d, xp: xp.where(d % 2 == 1, d + 1, d - 1),
        lambda d, xp: xp.where(d % 4 < 2, d - 2, d + 2),
    )


def pair_list(n, partner):
    pairs = []
    for d in range(n):
        p = int(partner(d, np))
        if 0 <= p < n and p != d:
            pairs.append((d, p))
    return pairs


LEVEL_BLOCKS = 3
PULSE_BLOCKS = 2


def level_block(levels):
    return levels // LEVEL_BLOCKS if levels % LEVEL_BLOCKS == 0 else levels


def full_spec(shape):
    return pl.BlockSpec(shape, lambda i: (0,) * len(shape))


def select_kernel(partners, hslot, slots_ref, values_ref, *refs):
    groups = len(partners)
    out_refs, select_ref = refs[:groups], refs[groups]
    me = lax.axis_index("cells")
    capacity = values_ref.shape[2]
    slots = slots_ref[...].astype(jnp.float32)
    peer_index = lax.broadcasted_iota(jnp.int32, slots.shape, 1)
    lanes = lax.broadcasted_iota(jnp.int32, (hslot, capacity), 1).astype(jnp.float32)
    for g, partner in enumerate(partners):
        peer = partner(me, jnp)
        column = jnp.sum(jnp.where(peer_index == peer, slots, 0.0), axis=1, keepdims=True)
        select_ref[g * hslot : (g + 1) * hslot, :] = (lanes == column).astype(jnp.float32)
    select = select_ref[...]
    for level in range(values_ref.shape[0]):
        block = lax.dot_general(
            select, values_ref[level], NT, precision=HIGHEST, preferred_element_type=jnp.float32
        )
        for g in range(groups):
            out_refs[g][level] = block[g * hslot : (g + 1) * hslot]


def gather_send(values, slots, partners, hslot):
    levels, pulses, capacity = values.shape
    groups = len(partners)
    shapes = [jax.ShapeDtypeStruct((levels, hslot, pulses), jnp.float32)] * groups
    shapes.append(jax.ShapeDtypeStruct((groups * hslot, capacity), jnp.float32))
    outs = pl.pallas_call(
        functools.partial(select_kernel, partners, hslot),
        out_shape=shapes,
        interpret=INTERPRET,
        name="gather_send",
    )(slots, values)
    return outs[:groups], outs[groups]


def local_kernel(values_ref, local_ref, mixing_ref, out_ref):
    levels = values_ref.shape[0]
    for level in range(levels):
        v = values_ref[level]
        x = v + jnp.dot(
            v, local_ref[level], precision=HIGHEST, preferred_element_type=jnp.float32
        )
        if level + 1 < levels:
            x = x + mixing_ref[level : level + 1, :] * (values_ref[level + 1] - v)
        if level > 0:
            x = x - mixing_ref[level - 1 : level, :] * (v - values_ref[level - 1])
        out_ref[level] = x


def local_part(values, matrix, mixing):
    levels, pulses, capacity = values.shape
    pb = pulses // PULSE_BLOCKS if pulses % (8 * PULSE_BLOCKS) == 0 else pulses
    value_spec = pl.BlockSpec((levels, pb, capacity), lambda i: (0, i, 0))
    return pl.pallas_call(
        local_kernel,
        out_shape=jax.ShapeDtypeStruct(values.shape, jnp.float32),
        grid=(pulses // pb,),
        in_specs=[
            value_spec,
            pl.BlockSpec((levels, capacity, capacity), lambda i: (0, 0, 0)),
            full_spec(mixing.shape),
        ],
        out_specs=value_spec,
        interpret=INTERPRET,
        name="local_part",
    )(values, matrix, mixing)


def finish_kernel(groups, hslot, mode, *refs):
    send = mode == "send"
    partial_ref = refs[0]
    incoming = refs[1 : 1 + groups]
    remote_refs = refs[1 + groups : 1 + 2 * groups]
    deposition_ref, count_ref, select_ref = refs[1 + 2 * groups : 4 + 2 * groups]
    rest = refs[4 + 2 * groups :]
    if mode == "local":
        local_ref, mixing_ref, out_ref, values_ref = rest
    elif send:
        out_ref, send_refs = None, rest
    else:
        (out_ref,) = rest
    lb = partial_ref.shape[0]
    first = 0
    capacity = partial_ref.shape[2]
    living = lax.broadcasted_iota(jnp.int32, (1, capacity), 1) < count_ref[...]
    for level in range(lb):
        received = jnp.concatenate([incoming[g][level] for g in range(groups)], axis=0)
        weights = jnp.concatenate([remote_refs[g][level] for g in range(groups)], axis=0)
        far = lax.dot_general(
            received,
            weights,
            TN,
            precision=HIGHEST,
            preferred_element_type=jnp.float32,
        )
        keep = 1.0 - deposition_ref[first + level : first + level + 1, :]
        x = (partial_ref[level] + far) * keep
        x = jnp.where(living, x, 0.0)
        if mode == "local":
            values_ref[level] = x
        elif not send:
            out_ref[level] = x
        if send:
            block = lax.dot_general(
                select_ref[...], x, NT, precision=HIGHEST, preferred_element_type=jnp.float32
            )
            for g in range(groups):
                send_refs[g][level] = block[g * hslot : (g + 1) * hslot]
    if mode == "local":
        local_kernel(values_ref, local_ref, mixing_ref, out_ref)


def finish(partial, incoming, matrix, deposition, count, select, mode, mixing=None):
    levels, pulses, capacity = partial.shape
    groups = len(incoming)
    hslot = incoming[0].shape[1]
    if mode == "send":
        shapes = [jax.ShapeDtypeStruct((levels, hslot, pulses), jnp.float32)] * groups
    else:
        shapes = [jax.ShapeDtypeStruct(partial.shape, jnp.float32)]
    operands = [partial, *incoming, *([matrix] * groups), deposition, count, select]
    specs = [full_spec(x.shape) for x in operands]
    for g in range(groups):
        block = capacity // hslot + g
        specs[1 + groups + g] = pl.BlockSpec(
            (levels, hslot, capacity), lambda i, block=block: (0, block, 0)
        )
    scratch = []
    if mode == "local":
        operands += [matrix, mixing]
        specs += [pl.BlockSpec((levels, capacity, capacity), lambda i: (0, 0, 0)), full_spec(mixing.shape)]
        scratch = [pltpu.VMEM(partial.shape, jnp.float32)]
    outs = pl.pallas_call(
        functools.partial(finish_kernel, groups, hslot, mode),
        out_shape=shapes,
        grid=(1,),
        in_specs=specs,
        out_specs=[full_spec(x.shape) for x in shapes],
        scratch_shapes=scratch,
        interpret=INTERPRET,
        name="finish_" + mode,
    )(*operands)
    return outs


def per_device(
    n, concentration, flux_weight, vertical_mixing, deposition, halo_index, send_cells, live_count
):
    levels, pulses, capacity = concentration.shape
    hslot = send_cells.shape[2]
    nbr = flux_weight.shape[0]
    partners = pairings(n)
    groups = len(partners)
    me = lax.axis_index("cells")
    f32 = jnp.float32

    lanes = jnp.arange(capacity, dtype=jnp.int32)
    values = concentration
    outgoing, select = gather_send(values, send_cells[0].T, partners, hslot)

    beyond = halo_index - capacity
    sender = beyond // hslot
    place = beyond % hslot
    row = jnp.where(beyond < 0, halo_index, -1)
    for g, partner in enumerate(partners):
        row = jnp.where(
            (beyond >= 0) & (sender == partner(me, jnp)), capacity + g * hslot + place, row
        )
    slots = jnp.arange(capacity + groups * hslot, dtype=jnp.int32)[:, None]
    diagonal = (slots == lanes[None, :]).astype(f32)
    matrix = sum(
        flux_weight[k][:, None, :] * ((row[k][None, :] == slots).astype(f32) - diagonal)[None]
        for k in range(nbr)
    )
    count = live_count.reshape(1, 1)

    partial = local_part(values, matrix, vertical_mixing)
    for sweep in range(STEPS):
        incoming = [
            lax.ppermute(outgoing[g], "cells", perm=pair_list(n, partner))
            for g, partner in enumerate(partners)
        ]
        common = (partial, incoming, matrix, deposition, count, select)
        if sweep + 1 < STEPS:
            outgoing = finish(*common, "send")
            partial = finish(*common, "local", vertical_mixing)[0]
        else:
            values = finish(*common, "final")[0]
    return values


def solution(mesh):
    n = mesh.shape["cells"]
    in_specs = (
        P(None, None, "cells"),
        P(None, None, "cells"),
        P(None, "cells"),
        P(None, "cells"),
        P(None, "cells"),
        P("cells", None, None),
        P("cells"),
    )
    out_specs = P(None, None, "cells")

    def body(*args):
        return per_device(n, *args)

    return jax.shard_map(body, mesh=mesh, in_specs=in_specs, out_specs=out_specs, check_vma=False)
```

```python
import functools

import jax
import numpy as np
import jax.numpy as jnp
from jax import lax
from jax.experimental import pallas as pl
from jax.sharding import PartitionSpec as P

STEPS = 2
HIGHEST = lax.Precision.HIGHEST
INTERPRET = False
NT = (((1,), (1,)), ((), ()))
TN = (((0,), (0,)), ((), ()))


def pairings(n):
    half = n // 2
    return (
        lambda d, xp: d ^ 1,
        lambda d, xp: xp.where(d % 4 < 2, d + 2, d - 2),
        lambda d, xp: (d + half) % n,
        lambda d, xp: xp.where(d % 2 == 1, d + 1, d - 1),
        lambda d, xp: xp.where(d % 4 < 2, d - 2, d + 2),
    )


def pair_list(n, partner):
    pairs = []
    for d in range(n):
        p = int(partner(d, np))
        if 0 <= p < n and p != d:
            pairs.append((d, p))
    return pairs


LEVEL_BLOCKS = 3
PULSE_BLOCKS = 2


def level_block(levels):
    return levels // LEVEL_BLOCKS if levels % LEVEL_BLOCKS == 0 else levels


def full_spec(shape):
    return pl.BlockSpec(shape, lambda i: (0,) * len(shape))


def select_rows(select, values):
    picker = select.astype(jnp.bfloat16)
    high = values.astype(jnp.bfloat16)
    rest = values - high.astype(jnp.float32)
    middle = rest.astype(jnp.bfloat16)
    low = (rest - middle.astype(jnp.float32)).astype(jnp.bfloat16)
    return sum(
        lax.dot_general(picker, part, NT, preferred_element_type=jnp.float32)
        for part in (high, middle, low)
    )


def select_kernel(partners, hslot, slots_ref, values_ref, *refs):
    groups = len(partners)
    out_refs, select_ref = refs[:groups], refs[groups]
    me = lax.axis_index("cells")
    capacity = values_ref.shape[2]
    slots = slots_ref[...].astype(jnp.float32)
    peer_index = lax.broadcasted_iota(jnp.int32, slots.shape, 1)
    lanes = lax.broadcasted_iota(jnp.int32, (hslot, capacity), 1).astype(jnp.float32)
    for g, partner in enumerate(partners):
        peer = partner(me, jnp)
        column = jnp.sum(jnp.where(peer_index == peer, slots, 0.0), axis=1, keepdims=True)
        select_ref[g * hslot : (g + 1) * hslot, :] = (lanes == column).astype(jnp.float32)
    select = select_ref[...]
    for level in range(values_ref.shape[0]):
        block = select_rows(select, values_ref[level])
        for g in range(groups):
            out_refs[g][level] = block[g * hslot : (g + 1) * hslot]


def gather_send(values, slots, partners, hslot):
    levels, pulses, capacity = values.shape
    groups = len(partners)
    shapes = [jax.ShapeDtypeStruct((levels, hslot, pulses), jnp.float32)] * groups
    shapes.append(jax.ShapeDtypeStruct((groups * hslot, capacity), jnp.float32))
    outs = pl.pallas_call(
        functools.partial(select_kernel, partners, hslot),
        out_shape=shapes,
        interpret=INTERPRET,
        name="gather_send",
    )(slots, values)
    return outs[:groups], outs[groups]


def local_kernel(values_ref, local_ref, mixing_ref, out_ref):
    levels = values_ref.shape[0]
    for level in range(levels):
        v = values_ref[level]
        x = v + jnp.dot(
            v, local_ref[level], precision=HIGHEST, preferred_element_type=jnp.float32
        )
        if level + 1 < levels:
            x = x + mixing_ref[level : level + 1, :] * (values_ref[level + 1] - v)
        if level > 0:
            x = x - mixing_ref[level - 1 : level, :] * (v - values_ref[level - 1])
        out_ref[level] = x


def local_part(values, matrix, mixing):
    levels, pulses, capacity = values.shape
    pb = pulses // PULSE_BLOCKS if pulses % (8 * PULSE_BLOCKS) == 0 else pulses
    value_spec = pl.BlockSpec((levels, pb, capacity), lambda i: (0, i, 0))
    return pl.pallas_call(
        local_kernel,
        out_shape=jax.ShapeDtypeStruct(values.shape, jnp.float32),
        grid=(pulses // pb,),
        in_specs=[
            value_spec,
            pl.BlockSpec((levels, capacity, capacity), lambda i: (0, 0, 0)),
            full_spec(mixing.shape),
        ],
        out_specs=value_spec,
        interpret=INTERPRET,
        name="local_part",
    )(values, matrix, mixing)


def finish_kernel(groups, hslot, send, *refs):
    partial_ref = refs[0]
    incoming = refs[1 : 1 + groups]
    remote_refs = refs[1 + groups : 1 + 2 * groups]
    deposition_ref, count_ref, select_ref = refs[1 + 2 * groups : 4 + 2 * groups]
    out_ref = refs[4 + 2 * groups]
    send_refs = refs[5 + 2 * groups :]
    lb = partial_ref.shape[0]
    first = 0
    capacity = partial_ref.shape[2]
    living = lax.broadcasted_iota(jnp.int32, (1, capacity), 1) < count_ref[...]
    for level in range(lb):
        received = jnp.concatenate([incoming[g][level] for g in range(groups)], axis=0)
        weights = jnp.concatenate([remote_refs[g][level] for g in range(groups)], axis=0)
        far = lax.dot_general(
            received,
            weights,
            TN,
            precision=HIGHEST,
            preferred_element_type=jnp.float32,
        )
        keep = 1.0 - deposition_ref[first + level : first + level + 1, :]
        x = (partial_ref[level] + far) * keep
        x = jnp.where(living, x, 0.0)
        out_ref[level] = x
        if send:
            block = select_rows(select_ref[...], x)
            for g in range(groups):
                send_refs[g][level] = block[g * hslot : (g + 1) * hslot]


def finish(partial, incoming, matrix, deposition, count, select, send):
    levels, pulses, capacity = partial.shape
    groups = len(incoming)
    hslot = incoming[0].shape[1]
    shapes = [jax.ShapeDtypeStruct(partial.shape, jnp.float32)]
    if send:
        shapes += [jax.ShapeDtypeStruct((levels, hslot, pulses), jnp.float32)] * groups
    operands = [partial, *incoming, *([matrix] * groups), deposition, count, select]
    specs = [full_spec(x.shape) for x in operands]
    for g in range(groups):
        block = capacity // hslot + g
        specs[1 + groups + g] = pl.BlockSpec(
            (levels, hslot, capacity), lambda i, block=block: (0, block, 0)
        )
    outs = pl.pallas_call(
        functools.partial(finish_kernel, groups, hslot, send),
        out_shape=shapes,
        grid=(1,),
        in_specs=specs,
        out_specs=[full_spec(x.shape) for x in shapes],
        interpret=INTERPRET,
        name="finish_send" if send else "finish",
    )(*operands)
    return outs[0], outs[1:]


def per_device(
    n, concentration, flux_weight, vertical_mixing, deposition, halo_index, send_cells, live_count
):
    levels, pulses, capacity = concentration.shape
    hslot = send_cells.shape[2]
    nbr = flux_weight.shape[0]
    partners = pairings(n)
    groups = len(partners)
    me = lax.axis_index("cells")
    f32 = jnp.float32

    lanes = jnp.arange(capacity, dtype=jnp.int32)
    values = concentration
    outgoing, select = gather_send(values, send_cells[0].T, partners, hslot)

    beyond = halo_index - capacity
    sender = beyond // hslot
    place = beyond % hslot
    row = jnp.where(beyond < 0, halo_index, -1)
    for g, partner in enumerate(partners):
        row = jnp.where(
            (beyond >= 0) & (sender == partner(me, jnp)), capacity + g * hslot + place, row
        )
    slots = jnp.arange(capacity + groups * hslot, dtype=jnp.int32)[:, None]
    diagonal = (slots == lanes[None, :]).astype(f32)
    matrix = sum(
        flux_weight[k][:, None, :] * ((row[k][None, :] == slots).astype(f32) - diagonal)[None]
        for k in range(nbr)
    )
    count = live_count.reshape(1, 1)

    for sweep in range(STEPS):
        incoming = [
            lax.ppermute(outgoing[g], "cells", perm=pair_list(n, partner))
            for g, partner in enumerate(partners)
        ]
        partial = local_part(values, matrix, vertical_mixing)
        values, outgoing = finish(
            partial, incoming, matrix, deposition, count, select, sweep + 1 < STEPS
        )
    return values


def solution(mesh):
    n = mesh.shape["cells"]
    in_specs = (
        P(None, None, "cells"),
        P(None, None, "cells"),
        P(None, "cells"),
        P(None, "cells"),
        P(None, "cells"),
        P("cells", None, None),
        P("cells"),
    )
    out_specs = P(None, None, "cells")

    def body(*args):
        return per_device(n, *args)

    return jax.shard_map(body, mesh=mesh, in_specs=in_specs, out_specs=out_specs, check_vma=False)
```

```python
import functools

import jax
import numpy as np
import jax.numpy as jnp
from jax import lax
from jax.experimental import pallas as pl
from jax.sharding import PartitionSpec as P

STEPS = 2
HIGHEST = lax.Precision.HIGHEST
INTERPRET = False
NT = (((1,), (1,)), ((), ()))
TN = (((0,), (0,)), ((), ()))


def pairings(n):
    half = n // 2
    return (
        lambda d, xp: d ^ 1,
        lambda d, xp: xp.where(d % 4 < 2, d + 2, d - 2),
        lambda d, xp: (d + half) % n,
        lambda d, xp: xp.where(d % 2 == 1, d + 1, d - 1),
        lambda d, xp: xp.where(d % 4 < 2, d - 2, d + 2),
    )


def pair_list(n, partner):
    pairs = []
    for d in range(n):
        p = int(partner(d, np))
        if 0 <= p < n and p != d:
            pairs.append((d, p))
    return pairs


LEVEL_BLOCKS = 3
PULSE_BLOCKS = 2


def level_block(levels):
    return levels // LEVEL_BLOCKS if levels % LEVEL_BLOCKS == 0 else levels


def full_spec(shape):
    return pl.BlockSpec(shape, lambda i: (0,) * len(shape))


def select_kernel(partners, hslot, slots_ref, values_ref, *refs):
    groups = len(partners)
    out_refs, select_ref = refs[:groups], refs[groups]
    me = lax.axis_index("cells")
    capacity = values_ref.shape[2]
    slots = slots_ref[...].astype(jnp.float32)
    peer_index = lax.broadcasted_iota(jnp.int32, slots.shape, 1)
    lanes = lax.broadcasted_iota(jnp.int32, (hslot, capacity), 1).astype(jnp.float32)
    for g, partner in enumerate(partners):
        peer = partner(me, jnp)
        column = jnp.sum(jnp.where(peer_index == peer, slots, 0.0), axis=1, keepdims=True)
        select_ref[g * hslot : (g + 1) * hslot, :] = (lanes == column).astype(jnp.float32)
    select = select_ref[...]
    for level in range(values_ref.shape[0]):
        block = lax.dot_general(
            select, values_ref[level], NT, precision=HIGHEST, preferred_element_type=jnp.float32
        )
        for g in range(groups):
            out_refs[g][level] = block[g * hslot : (g + 1) * hslot]


def gather_send(values, slots, partners, hslot):
    levels, pulses, capacity = values.shape
    groups = len(partners)
    shapes = [jax.ShapeDtypeStruct((levels, hslot, pulses), jnp.float32)] * groups
    shapes.append(jax.ShapeDtypeStruct((groups * hslot, capacity), jnp.float32))
    outs = pl.pallas_call(
        functools.partial(select_kernel, partners, hslot),
        out_shape=shapes,
        interpret=INTERPRET,
        name="gather_send",
    )(slots, values)
    return outs[:groups], outs[groups]


def local_kernel(values_ref, local_ref, mixing_ref, out_ref):
    levels = values_ref.shape[0]
    for level in range(levels):
        v = values_ref[level]
        x = v + jnp.dot(
            v, local_ref[level], precision=HIGHEST, preferred_element_type=jnp.float32
        )
        if level + 1 < levels:
            x = x + mixing_ref[level : level + 1, :] * (values_ref[level + 1] - v)
        if level > 0:
            x = x - mixing_ref[level - 1 : level, :] * (v - values_ref[level - 1])
        out_ref[level] = x


def local_part(values, matrix, mixing):
    levels, pulses, capacity = values.shape
    pb = pulses // PULSE_BLOCKS if pulses % (8 * PULSE_BLOCKS) == 0 else pulses
    value_spec = pl.BlockSpec((levels, pb, capacity), lambda i: (0, i, 0))
    return pl.pallas_call(
        local_kernel,
        out_shape=jax.ShapeDtypeStruct(values.shape, jnp.float32),
        grid=(pulses // pb,),
        in_specs=[
            value_spec,
            pl.BlockSpec((levels, capacity, capacity), lambda i: (0, 0, 0)),
            full_spec(mixing.shape),
        ],
        out_specs=value_spec,
        interpret=INTERPRET,
        name="local_part",
    )(values, matrix, mixing)


def finish_kernel(groups, hslot, send, *refs):
    partial_ref = refs[0]
    incoming = refs[1 : 1 + groups]
    remote_ref, deposition_ref, count_ref, select_ref = refs[1 + groups : 5 + groups]
    out_ref = refs[5 + groups]
    send_refs = refs[6 + groups :]
    lb = partial_ref.shape[0]
    first = 0
    capacity = partial_ref.shape[2]
    living = lax.broadcasted_iota(jnp.int32, (1, capacity), 1) < count_ref[...]
    for level in range(lb):
        received = jnp.concatenate([incoming[g][level] for g in range(groups)], axis=0)
        far = jnp.dot(
            remote_ref[level], received, precision=HIGHEST, preferred_element_type=jnp.float32
        ).T
        keep = 1.0 - deposition_ref[first + level : first + level + 1, :]
        x = (partial_ref[level] + far) * keep
        x = jnp.where(living, x, 0.0)
        out_ref[level] = x
        if send:
            block = lax.dot_general(
                select_ref[...], x, NT, precision=HIGHEST, preferred_element_type=jnp.float32
            )
            for g in range(groups):
                send_refs[g][level] = block[g * hslot : (g + 1) * hslot]


def finish(partial, incoming, matrix, deposition, count, select, send):
    levels, pulses, capacity = partial.shape
    groups = len(incoming)
    hslot = incoming[0].shape[1]
    shapes = [jax.ShapeDtypeStruct(partial.shape, jnp.float32)]
    if send:
        shapes += [jax.ShapeDtypeStruct((levels, hslot, pulses), jnp.float32)] * groups
    operands = [partial, *incoming, matrix, deposition, count, select]
    specs = [full_spec(x.shape) for x in operands]
    outs = pl.pallas_call(
        functools.partial(finish_kernel, groups, hslot, send),
        out_shape=shapes,
        grid=(1,),
        in_specs=specs,
        out_specs=[full_spec(x.shape) for x in shapes],
        interpret=INTERPRET,
        name="finish_send" if send else "finish",
    )(*operands)
    return outs[0], outs[1:]


def per_device(
    n, concentration, flux_weight, vertical_mixing, deposition, halo_index, send_cells, live_count
):
    levels, pulses, capacity = concentration.shape
    hslot = send_cells.shape[2]
    nbr = flux_weight.shape[0]
    partners = pairings(n)
    groups = len(partners)
    me = lax.axis_index("cells")
    f32 = jnp.float32

    lanes = jnp.arange(capacity, dtype=jnp.int32)
    values = concentration
    outgoing, select = gather_send(values, send_cells[0].T, partners, hslot)

    beyond = halo_index - capacity
    sender = beyond // hslot
    place = beyond % hslot
    row = jnp.where(beyond < 0, halo_index, -1)
    for g, partner in enumerate(partners):
        row = jnp.where(
            (beyond >= 0) & (sender == partner(me, jnp)), capacity + g * hslot + place, row
        )
    slots = jnp.arange(capacity + groups * hslot, dtype=jnp.int32)[:, None]
    diagonal = (slots == lanes[None, :]).astype(f32)
    matrix = sum(
        flux_weight[k][:, None, :] * ((row[k][None, :] == slots).astype(f32) - diagonal)[None]
        for k in range(nbr)
    )
    received_slots = jnp.arange(groups * hslot, dtype=jnp.int32)[None, :]
    remote_t = sum(
        flux_weight[k][:, :, None] * (row[k][:, None] - capacity == received_slots).astype(f32)[None]
        for k in range(nbr)
    )
    count = live_count.reshape(1, 1)

    for sweep in range(STEPS):
        incoming = [
            lax.ppermute(outgoing[g], "cells", perm=pair_list(n, partner))
            for g, partner in enumerate(partners)
        ]
        partial = local_part(values, matrix, vertical_mixing)
        values, outgoing = finish(
            partial, incoming, remote_t, deposition, count, select, sweep + 1 < STEPS
        )
    return values


def solution(mesh):
    n = mesh.shape["cells"]
    in_specs = (
        P(None, None, "cells"),
        P(None, None, "cells"),
        P(None, "cells"),
        P(None, "cells"),
        P(None, "cells"),
        P("cells", None, None),
        P("cells"),
    )
    out_specs = P(None, None, "cells")

    def body(*args):
        return per_device(n, *args)

    return jax.shard_map(body, mesh=mesh, in_specs=in_specs, out_specs=out_specs, check_vma=False)
```

```python
import functools

import jax
import numpy as np
import jax.numpy as jnp
from jax import lax
from jax.experimental import pallas as pl
from jax.sharding import PartitionSpec as P

STEPS = 2
HIGHEST = lax.Precision.HIGHEST
HIGH = lax.Precision.HIGH
INTERPRET = False
NT = (((1,), (1,)), ((), ()))
TN = (((0,), (0,)), ((), ()))


def pairings(n):
    half = n // 2
    return (
        lambda d, xp: d ^ 1,
        lambda d, xp: xp.where(d % 4 < 2, d + 2, d - 2),
        lambda d, xp: (d + half) % n,
        lambda d, xp: xp.where(d % 2 == 1, d + 1, d - 1),
        lambda d, xp: xp.where(d % 4 < 2, d - 2, d + 2),
    )


def pair_list(n, partner):
    pairs = []
    for d in range(n):
        p = int(partner(d, np))
        if 0 <= p < n and p != d:
            pairs.append((d, p))
    return pairs


LEVEL_BLOCKS = 3
PULSE_BLOCKS = 2


def level_block(levels):
    return levels // LEVEL_BLOCKS if levels % LEVEL_BLOCKS == 0 else levels


def full_spec(shape):
    return pl.BlockSpec(shape, lambda i: (0,) * len(shape))


def select_kernel(partners, hslot, slots_ref, values_ref, *refs):
    groups = len(partners)
    out_refs, select_ref = refs[:groups], refs[groups]
    me = lax.axis_index("cells")
    capacity = values_ref.shape[2]
    slots = slots_ref[...].astype(jnp.float32)
    peer_index = lax.broadcasted_iota(jnp.int32, slots.shape, 1)
    lanes = lax.broadcasted_iota(jnp.int32, (hslot, capacity), 1).astype(jnp.float32)
    for g, partner in enumerate(partners):
        peer = partner(me, jnp)
        column = jnp.sum(jnp.where(peer_index == peer, slots, 0.0), axis=1, keepdims=True)
        select_ref[g * hslot : (g + 1) * hslot, :] = (lanes == column).astype(jnp.float32)
    select = select_ref[...]
    for level in range(values_ref.shape[0]):
        block = lax.dot_general(
            select, values_ref[level], NT, precision=HIGH, preferred_element_type=jnp.float32
        )
        for g in range(groups):
            out_refs[g][level] = block[g * hslot : (g + 1) * hslot]


def gather_send(values, slots, partners, hslot):
    levels, pulses, capacity = values.shape
    groups = len(partners)
    shapes = [jax.ShapeDtypeStruct((levels, hslot, pulses), jnp.float32)] * groups
    shapes.append(jax.ShapeDtypeStruct((groups * hslot, capacity), jnp.float32))
    outs = pl.pallas_call(
        functools.partial(select_kernel, partners, hslot),
        out_shape=shapes,
        interpret=INTERPRET,
        name="gather_send",
    )(slots, values)
    return outs[:groups], outs[groups]


def local_kernel(values_ref, local_ref, mixing_ref, out_ref):
    levels = values_ref.shape[0]
    for level in range(levels):
        v = values_ref[level]
        x = v + jnp.dot(
            v, local_ref[level], precision=HIGHEST, preferred_element_type=jnp.float32
        )
        if level + 1 < levels:
            x = x + mixing_ref[level : level + 1, :] * (values_ref[level + 1] - v)
        if level > 0:
            x = x - mixing_ref[level - 1 : level, :] * (v - values_ref[level - 1])
        out_ref[level] = x


def local_part(values, matrix, mixing):
    levels, pulses, capacity = values.shape
    pb = pulses // PULSE_BLOCKS if pulses % (8 * PULSE_BLOCKS) == 0 else pulses
    value_spec = pl.BlockSpec((levels, pb, capacity), lambda i: (0, i, 0))
    return pl.pallas_call(
        local_kernel,
        out_shape=jax.ShapeDtypeStruct(values.shape, jnp.float32),
        grid=(pulses // pb,),
        in_specs=[
            value_spec,
            pl.BlockSpec((levels, capacity, capacity), lambda i: (0, 0, 0)),
            full_spec(mixing.shape),
        ],
        out_specs=value_spec,
        interpret=INTERPRET,
        name="local_part",
    )(values, matrix, mixing)


def finish_kernel(groups, hslot, send, *refs):
    partial_ref = refs[0]
    incoming = refs[1 : 1 + groups]
    remote_refs = refs[1 + groups : 1 + 2 * groups]
    deposition_ref, count_ref, select_ref = refs[1 + 2 * groups : 4 + 2 * groups]
    out_ref = refs[4 + 2 * groups]
    send_refs = refs[5 + 2 * groups :]
    lb = partial_ref.shape[0]
    first = 0
    capacity = partial_ref.shape[2]
    living = lax.broadcasted_iota(jnp.int32, (1, capacity), 1) < count_ref[...]
    for level in range(lb):
        received = jnp.concatenate([incoming[g][level] for g in range(groups)], axis=0)
        weights = jnp.concatenate([remote_refs[g][level] for g in range(groups)], axis=0)
        far = lax.dot_general(
            received,
            weights,
            TN,
            precision=HIGH,
            preferred_element_type=jnp.float32,
        )
        keep = 1.0 - deposition_ref[first + level : first + level + 1, :]
        x = (partial_ref[level] + far) * keep
        x = jnp.where(living, x, 0.0)
        out_ref[level] = x
        if send:
            block = lax.dot_general(
                select_ref[...], x, NT, precision=HIGH, preferred_element_type=jnp.float32
            )
            for g in range(groups):
                send_refs[g][level] = block[g * hslot : (g + 1) * hslot]


def finish(partial, incoming, matrix, deposition, count, select, send):
    levels, pulses, capacity = partial.shape
    groups = len(incoming)
    hslot = incoming[0].shape[1]
    shapes = [jax.ShapeDtypeStruct(partial.shape, jnp.float32)]
    if send:
        shapes += [jax.ShapeDtypeStruct((levels, hslot, pulses), jnp.float32)] * groups
    operands = [partial, *incoming, *([matrix] * groups), deposition, count, select]
    specs = [full_spec(x.shape) for x in operands]
    for g in range(groups):
        block = capacity // hslot + g
        specs[1 + groups + g] = pl.BlockSpec(
            (levels, hslot, capacity), lambda i, block=block: (0, block, 0)
        )
    outs = pl.pallas_call(
        functools.partial(finish_kernel, groups, hslot, send),
        out_shape=shapes,
        grid=(1,),
        in_specs=specs,
        out_specs=[full_spec(x.shape) for x in shapes],
        interpret=INTERPRET,
        name="finish_send" if send else "finish",
    )(*operands)
    return outs[0], outs[1:]


def per_device(
    n, concentration, flux_weight, vertical_mixing, deposition, halo_index, send_cells, live_count
):
    levels, pulses, capacity = concentration.shape
    hslot = send_cells.shape[2]
    nbr = flux_weight.shape[0]
    partners = pairings(n)
    groups = len(partners)
    me = lax.axis_index("cells")
    f32 = jnp.float32

    lanes = jnp.arange(capacity, dtype=jnp.int32)
    values = concentration
    outgoing, select = gather_send(values, send_cells[0].T, partners, hslot)

    beyond = halo_index - capacity
    sender = beyond // hslot
    place = beyond % hslot
    row = jnp.where(beyond < 0, halo_index, -1)
    for g, partner in enumerate(partners):
        row = jnp.where(
            (beyond >= 0) & (sender == partner(me, jnp)), capacity + g * hslot + place, row
        )
    slots = jnp.arange(capacity + groups * hslot, dtype=jnp.int32)[:, None]
    diagonal = (slots == lanes[None, :]).astype(f32)
    matrix = sum(
        flux_weight[k][:, None, :] * ((row[k][None, :] == slots).astype(f32) - diagonal)[None]
        for k in range(nbr)
    )
    count = live_count.reshape(1, 1)

    for sweep in range(STEPS):
        incoming = [
            lax.ppermute(outgoing[g], "cells", perm=pair_list(n, partner))
            for g, partner in enumerate(partners)
        ]
        partial = local_part(values, matrix, vertical_mixing)
        values, outgoing = finish(
            partial, incoming, matrix, deposition, count, select, sweep + 1 < STEPS
        )
    return values


def solution(mesh):
    n = mesh.shape["cells"]
    in_specs = (
        P(None, None, "cells"),
        P(None, None, "cells"),
        P(None, "cells"),
        P(None, "cells"),
        P(None, "cells"),
        P("cells", None, None),
        P("cells"),
    )
    out_specs = P(None, None, "cells")

    def body(*args):
        return per_device(n, *args)

    return jax.shard_map(body, mesh=mesh, in_specs=in_specs, out_specs=out_specs, check_vma=False)
```

```python
import functools

import jax
import numpy as np
import jax.numpy as jnp
from jax import lax
from jax.experimental import pallas as pl
from jax.sharding import PartitionSpec as P

STEPS = 2
HIGH = lax.Precision.HIGH
INTERPRET = False
NT = (((1,), (1,)), ((), ()))
TN = (((0,), (0,)), ((), ()))


def pairings(n):
    half = n // 2
    return (
        lambda d, xp: d ^ 1,
        lambda d, xp: xp.where(d % 4 < 2, d + 2, d - 2),
        lambda d, xp: (d + half) % n,
        lambda d, xp: xp.where(d % 2 == 1, d + 1, d - 1),
        lambda d, xp: xp.where(d % 4 < 2, d - 2, d + 2),
    )


def pair_list(n, partner):
    pairs = []
    for d in range(n):
        p = int(partner(d, np))
        if 0 <= p < n and p != d:
            pairs.append((d, p))
    return pairs


LEVEL_BLOCKS = 3
PULSE_BLOCKS = 2


def level_block(levels):
    return levels // LEVEL_BLOCKS if levels % LEVEL_BLOCKS == 0 else levels


def full_spec(shape):
    return pl.BlockSpec(shape, lambda i: (0,) * len(shape))


def select_kernel(partners, hslot, slots_ref, values_ref, *refs):
    groups = len(partners)
    out_refs, select_ref = refs[:groups], refs[groups]
    me = lax.axis_index("cells")
    capacity = values_ref.shape[2]
    slots = slots_ref[...].astype(jnp.float32)
    peer_index = lax.broadcasted_iota(jnp.int32, slots.shape, 1)
    lanes = lax.broadcasted_iota(jnp.int32, (hslot, capacity), 1).astype(jnp.float32)
    for g, partner in enumerate(partners):
        peer = partner(me, jnp)
        column = jnp.sum(jnp.where(peer_index == peer, slots, 0.0), axis=1, keepdims=True)
        select_ref[g * hslot : (g + 1) * hslot, :] = (lanes == column).astype(jnp.float32)
    select = select_ref[...]
    for level in range(values_ref.shape[0]):
        block = lax.dot_general(
            select, values_ref[level], NT, precision=HIGH, preferred_element_type=jnp.float32
        )
        for g in range(groups):
            out_refs[g][level] = block[g * hslot : (g + 1) * hslot]


def gather_send(values, slots, partners, hslot):
    levels, pulses, capacity = values.shape
    groups = len(partners)
    shapes = [jax.ShapeDtypeStruct((levels, hslot, pulses), jnp.float32)] * groups
    shapes.append(jax.ShapeDtypeStruct((groups * hslot, capacity), jnp.float32))
    outs = pl.pallas_call(
        functools.partial(select_kernel, partners, hslot),
        out_shape=shapes,
        interpret=INTERPRET,
        name="gather_send",
    )(slots, values)
    return outs[:groups], outs[groups]


def local_kernel(values_ref, local_ref, mixing_ref, out_ref):
    levels = values_ref.shape[0]
    for level in range(levels):
        v = values_ref[level]
        x = v + jnp.dot(
            v, local_ref[level], precision=HIGH, preferred_element_type=jnp.float32
        )
        if level + 1 < levels:
            x = x + mixing_ref[level : level + 1, :] * (values_ref[level + 1] - v)
        if level > 0:
            x = x - mixing_ref[level - 1 : level, :] * (v - values_ref[level - 1])
        out_ref[level] = x


def local_part(values, matrix, mixing):
    levels, pulses, capacity = values.shape
    pb = pulses // PULSE_BLOCKS if pulses % (8 * PULSE_BLOCKS) == 0 else pulses
    value_spec = pl.BlockSpec((levels, pb, capacity), lambda i: (0, i, 0))
    return pl.pallas_call(
        local_kernel,
        out_shape=jax.ShapeDtypeStruct(values.shape, jnp.float32),
        grid=(pulses // pb,),
        in_specs=[
            value_spec,
            pl.BlockSpec((levels, capacity, capacity), lambda i: (0, 0, 0)),
            full_spec(mixing.shape),
        ],
        out_specs=value_spec,
        interpret=INTERPRET,
        name="local_part",
    )(values, matrix, mixing)


def finish_kernel(groups, hslot, send, *refs):
    partial_ref = refs[0]
    incoming = refs[1 : 1 + groups]
    remote_refs = refs[1 + groups : 1 + 2 * groups]
    deposition_ref, count_ref, select_ref = refs[1 + 2 * groups : 4 + 2 * groups]
    out_ref = refs[4 + 2 * groups]
    send_refs = refs[5 + 2 * groups :]
    lb = partial_ref.shape[0]
    first = 0
    capacity = partial_ref.shape[2]
    living = lax.broadcasted_iota(jnp.int32, (1, capacity), 1) < count_ref[...]
    for level in range(lb):
        received = jnp.concatenate([incoming[g][level] for g in range(groups)], axis=0)
        weights = jnp.concatenate([remote_refs[g][level] for g in range(groups)], axis=0)
        far = lax.dot_general(
            received,
            weights,
            TN,
            precision=HIGH,
            preferred_element_type=jnp.float32,
        )
        keep = 1.0 - deposition_ref[first + level : first + level + 1, :]
        x = (partial_ref[level] + far) * keep
        x = jnp.where(living, x, 0.0)
        out_ref[level] = x
        if send:
            block = lax.dot_general(
                select_ref[...], x, NT, precision=HIGH, preferred_element_type=jnp.float32
            )
            for g in range(groups):
                send_refs[g][level] = block[g * hslot : (g + 1) * hslot]


def finish(partial, incoming, matrix, deposition, count, select, send):
    levels, pulses, capacity = partial.shape
    groups = len(incoming)
    hslot = incoming[0].shape[1]
    shapes = [jax.ShapeDtypeStruct(partial.shape, jnp.float32)]
    if send:
        shapes += [jax.ShapeDtypeStruct((levels, hslot, pulses), jnp.float32)] * groups
    operands = [partial, *incoming, *([matrix] * groups), deposition, count, select]
    specs = [full_spec(x.shape) for x in operands]
    for g in range(groups):
        block = capacity // hslot + g
        specs[1 + groups + g] = pl.BlockSpec(
            (levels, hslot, capacity), lambda i, block=block: (0, block, 0)
        )
    outs = pl.pallas_call(
        functools.partial(finish_kernel, groups, hslot, send),
        out_shape=shapes,
        grid=(1,),
        in_specs=specs,
        out_specs=[full_spec(x.shape) for x in shapes],
        interpret=INTERPRET,
        name="finish_send" if send else "finish",
    )(*operands)
    return outs[0], outs[1:]


def per_device(
    n, concentration, flux_weight, vertical_mixing, deposition, halo_index, send_cells, live_count
):
    levels, pulses, capacity = concentration.shape
    hslot = send_cells.shape[2]
    nbr = flux_weight.shape[0]
    partners = pairings(n)
    groups = len(partners)
    me = lax.axis_index("cells")
    f32 = jnp.float32

    lanes = jnp.arange(capacity, dtype=jnp.int32)
    values = concentration
    outgoing, select = gather_send(values, send_cells[0].T, partners, hslot)

    beyond = halo_index - capacity
    sender = beyond // hslot
    place = beyond % hslot
    row = jnp.where(beyond < 0, halo_index, -1)
    for g, partner in enumerate(partners):
        row = jnp.where(
            (beyond >= 0) & (sender == partner(me, jnp)), capacity + g * hslot + place, row
        )
    slots = jnp.arange(capacity + groups * hslot, dtype=jnp.int32)[:, None]
    diagonal = (slots == lanes[None, :]).astype(f32)
    matrix = sum(
        flux_weight[k][:, None, :] * ((row[k][None, :] == slots).astype(f32) - diagonal)[None]
        for k in range(nbr)
    )
    count = live_count.reshape(1, 1)

    for sweep in range(STEPS):
        incoming = [
            lax.ppermute(outgoing[g], "cells", perm=pair_list(n, partner))
            for g, partner in enumerate(partners)
        ]
        partial = local_part(values, matrix, vertical_mixing)
        values, outgoing = finish(
            partial, incoming, matrix, deposition, count, select, sweep + 1 < STEPS
        )
    return values


def solution(mesh):
    n = mesh.shape["cells"]
    in_specs = (
        P(None, None, "cells"),
        P(None, None, "cells"),
        P(None, "cells"),
        P(None, "cells"),
        P(None, "cells"),
        P("cells", None, None),
        P("cells"),
    )
    out_specs = P(None, None, "cells")

    def body(*args):
        return per_device(n, *args)

    return jax.shard_map(body, mesh=mesh, in_specs=in_specs, out_specs=out_specs, check_vma=False)
```

```python
import functools

import jax
import numpy as np
import jax.numpy as jnp
from jax import lax
from jax.experimental import pallas as pl
from jax.sharding import PartitionSpec as P

STEPS = 2
HIGH = lax.Precision.HIGH
INTERPRET = False
NT = (((1,), (1,)), ((), ()))
TN = (((0,), (0,)), ((), ()))


def pairings(n):
    half = n // 2
    return (
        lambda d, xp: d ^ 1,
        lambda d, xp: xp.where(d % 4 < 2, d + 2, d - 2),
        lambda d, xp: (d + half) % n,
        lambda d, xp: xp.where(d % 2 == 1, d + 1, d - 1),
        lambda d, xp: xp.where(d % 4 < 2, d - 2, d + 2),
    )


def pair_list(n, partner):
    pairs = []
    for d in range(n):
        p = int(partner(d, np))
        if 0 <= p < n and p != d:
            pairs.append((d, p))
    return pairs


LEVEL_BLOCKS = 3
PULSE_BLOCKS = 4


def level_block(levels):
    return levels // LEVEL_BLOCKS if levels % LEVEL_BLOCKS == 0 else levels


def full_spec(shape):
    return pl.BlockSpec(shape, lambda i: (0,) * len(shape))


def select_kernel(partners, hslot, slots_ref, values_ref, *refs):
    groups = len(partners)
    out_refs, select_ref = refs[:groups], refs[groups]
    me = lax.axis_index("cells")
    capacity = values_ref.shape[2]
    slots = slots_ref[...].astype(jnp.float32)
    peer_index = lax.broadcasted_iota(jnp.int32, slots.shape, 1)
    lanes = lax.broadcasted_iota(jnp.int32, (hslot, capacity), 1).astype(jnp.float32)
    for g, partner in enumerate(partners):
        peer = partner(me, jnp)
        column = jnp.sum(jnp.where(peer_index == peer, slots, 0.0), axis=1, keepdims=True)
        select_ref[g * hslot : (g + 1) * hslot, :] = (lanes == column).astype(jnp.float32)
    select = select_ref[...]
    for level in range(values_ref.shape[0]):
        block = lax.dot_general(
            select, values_ref[level], NT, precision=HIGH, preferred_element_type=jnp.float32
        )
        for g in range(groups):
            out_refs[g][level] = block[g * hslot : (g + 1) * hslot]


def gather_send(values, slots, partners, hslot):
    levels, pulses, capacity = values.shape
    groups = len(partners)
    shapes = [jax.ShapeDtypeStruct((levels, hslot, pulses), jnp.float32)] * groups
    shapes.append(jax.ShapeDtypeStruct((groups * hslot, capacity), jnp.float32))
    outs = pl.pallas_call(
        functools.partial(select_kernel, partners, hslot),
        out_shape=shapes,
        interpret=INTERPRET,
        name="gather_send",
    )(slots, values)
    return outs[:groups], outs[groups]


def local_kernel(values_ref, local_ref, mixing_ref, out_ref):
    levels = values_ref.shape[0]
    for level in range(levels):
        v = values_ref[level]
        x = v + jnp.dot(
            v, local_ref[level], precision=HIGH, preferred_element_type=jnp.float32
        )
        if level + 1 < levels:
            x = x + mixing_ref[level : level + 1, :] * (values_ref[level + 1] - v)
        if level > 0:
            x = x - mixing_ref[level - 1 : level, :] * (v - values_ref[level - 1])
        out_ref[level] = x


def local_part(values, matrix, mixing):
    levels, pulses, capacity = values.shape
    pb = pulses // PULSE_BLOCKS if pulses % (8 * PULSE_BLOCKS) == 0 else pulses
    value_spec = pl.BlockSpec((levels, pb, capacity), lambda i: (0, i, 0))
    return pl.pallas_call(
        local_kernel,
        out_shape=jax.ShapeDtypeStruct(values.shape, jnp.float32),
        grid=(pulses // pb,),
        in_specs=[
            value_spec,
            pl.BlockSpec((levels, capacity, capacity), lambda i: (0, 0, 0)),
            full_spec(mixing.shape),
        ],
        out_specs=value_spec,
        interpret=INTERPRET,
        name="local_part",
    )(values, matrix, mixing)


def finish_kernel(groups, hslot, send, *refs):
    partial_ref = refs[0]
    incoming = refs[1 : 1 + groups]
    remote_refs = refs[1 + groups : 1 + 2 * groups]
    deposition_ref, count_ref, select_ref = refs[1 + 2 * groups : 4 + 2 * groups]
    out_ref = refs[4 + 2 * groups]
    send_refs = refs[5 + 2 * groups :]
    lb = partial_ref.shape[0]
    first = 0
    capacity = partial_ref.shape[2]
    living = lax.broadcasted_iota(jnp.int32, (1, capacity), 1) < count_ref[...]
    for level in range(lb):
        received = jnp.concatenate([incoming[g][level] for g in range(groups)], axis=0)
        weights = jnp.concatenate([remote_refs[g][level] for g in range(groups)], axis=0)
        far = lax.dot_general(
            received,
            weights,
            TN,
            precision=HIGH,
            preferred_element_type=jnp.float32,
        )
        keep = 1.0 - deposition_ref[first + level : first + level + 1, :]
        x = (partial_ref[level] + far) * keep
        x = jnp.where(living, x, 0.0)
        out_ref[level] = x
        if send:
            block = lax.dot_general(
                select_ref[...], x, NT, precision=HIGH, preferred_element_type=jnp.float32
            )
            for g in range(groups):
                send_refs[g][level] = block[g * hslot : (g + 1) * hslot]


def finish(partial, incoming, matrix, deposition, count, select, send):
    levels, pulses, capacity = partial.shape
    groups = len(incoming)
    hslot = incoming[0].shape[1]
    shapes = [jax.ShapeDtypeStruct(partial.shape, jnp.float32)]
    if send:
        shapes += [jax.ShapeDtypeStruct((levels, hslot, pulses), jnp.float32)] * groups
    operands = [partial, *incoming, *([matrix] * groups), deposition, count, select]
    specs = [full_spec(x.shape) for x in operands]
    for g in range(groups):
        block = capacity // hslot + g
        specs[1 + groups + g] = pl.BlockSpec(
            (levels, hslot, capacity), lambda i, block=block: (0, block, 0)
        )
    outs = pl.pallas_call(
        functools.partial(finish_kernel, groups, hslot, send),
        out_shape=shapes,
        grid=(1,),
        in_specs=specs,
        out_specs=[full_spec(x.shape) for x in shapes],
        interpret=INTERPRET,
        name="finish_send" if send else "finish",
    )(*operands)
    return outs[0], outs[1:]


def per_device(
    n, concentration, flux_weight, vertical_mixing, deposition, halo_index, send_cells, live_count
):
    levels, pulses, capacity = concentration.shape
    hslot = send_cells.shape[2]
    nbr = flux_weight.shape[0]
    partners = pairings(n)
    groups = len(partners)
    me = lax.axis_index("cells")
    f32 = jnp.float32

    lanes = jnp.arange(capacity, dtype=jnp.int32)
    values = concentration
    outgoing, select = gather_send(values, send_cells[0].T, partners, hslot)

    beyond = halo_index - capacity
    sender = beyond // hslot
    place = beyond % hslot
    row = jnp.where(beyond < 0, halo_index, -1)
    for g, partner in enumerate(partners):
        row = jnp.where(
            (beyond >= 0) & (sender == partner(me, jnp)), capacity + g * hslot + place, row
        )
    slots = jnp.arange(capacity + groups * hslot, dtype=jnp.int32)[:, None]
    diagonal = (slots == lanes[None, :]).astype(f32)
    matrix = sum(
        flux_weight[k][:, None, :] * ((row[k][None, :] == slots).astype(f32) - diagonal)[None]
        for k in range(nbr)
    )
    count = live_count.reshape(1, 1)

    for sweep in range(STEPS):
        incoming = [
            lax.ppermute(outgoing[g], "cells", perm=pair_list(n, partner))
            for g, partner in enumerate(partners)
        ]
        partial = local_part(values, matrix, vertical_mixing)
        values, outgoing = finish(
            partial, incoming, matrix, deposition, count, select, sweep + 1 < STEPS
        )
    return values


def solution(mesh):
    n = mesh.shape["cells"]
    in_specs = (
        P(None, None, "cells"),
        P(None, None, "cells"),
        P(None, "cells"),
        P(None, "cells"),
        P(None, "cells"),
        P("cells", None, None),
        P("cells"),
    )
    out_specs = P(None, None, "cells")

    def body(*args):
        return per_device(n, *args)

    return jax.shard_map(body, mesh=mesh, in_specs=in_specs, out_specs=out_specs, check_vma=False)
```

```python
import functools

import jax
import numpy as np
import jax.numpy as jnp
from jax import lax
from jax.experimental import pallas as pl
from jax.sharding import PartitionSpec as P

STEPS = 2
HIGH = lax.Precision.HIGH
INTERPRET = False
NT = (((1,), (1,)), ((), ()))
TN = (((0,), (0,)), ((), ()))


def pairings(n):
    half = n // 2
    return (
        lambda d, xp: d ^ 1,
        lambda d, xp: xp.where(d % 4 < 2, d + 2, d - 2),
        lambda d, xp: (d + half) % n,
        lambda d, xp: xp.where(d % 2 == 1, d + 1, d - 1),
        lambda d, xp: xp.where(d % 4 < 2, d - 2, d + 2),
    )


def pair_list(n, partner):
    pairs = []
    for d in range(n):
        p = int(partner(d, np))
        if 0 <= p < n and p != d:
            pairs.append((d, p))
    return pairs


LEVEL_BLOCKS = 3
PULSE_BLOCKS = 1


def level_block(levels):
    return levels // LEVEL_BLOCKS if levels % LEVEL_BLOCKS == 0 else levels


def full_spec(shape):
    return pl.BlockSpec(shape, lambda i: (0,) * len(shape))


def select_kernel(partners, hslot, slots_ref, values_ref, *refs):
    groups = len(partners)
    out_refs, select_ref = refs[:groups], refs[groups]
    me = lax.axis_index("cells")
    capacity = values_ref.shape[2]
    slots = slots_ref[...].astype(jnp.float32)
    peer_index = lax.broadcasted_iota(jnp.int32, slots.shape, 1)
    lanes = lax.broadcasted_iota(jnp.int32, (hslot, capacity), 1).astype(jnp.float32)
    for g, partner in enumerate(partners):
        peer = partner(me, jnp)
        column = jnp.sum(jnp.where(peer_index == peer, slots, 0.0), axis=1, keepdims=True)
        select_ref[g * hslot : (g + 1) * hslot, :] = (lanes == column).astype(jnp.float32)
    select = select_ref[...]
    for level in range(values_ref.shape[0]):
        block = lax.dot_general(
            select, values_ref[level], NT, precision=HIGH, preferred_element_type=jnp.float32
        )
        for g in range(groups):
            out_refs[g][level] = block[g * hslot : (g + 1) * hslot]


def gather_send(values, slots, partners, hslot):
    levels, pulses, capacity = values.shape
    groups = len(partners)
    shapes = [jax.ShapeDtypeStruct((levels, hslot, pulses), jnp.float32)] * groups
    shapes.append(jax.ShapeDtypeStruct((groups * hslot, capacity), jnp.float32))
    outs = pl.pallas_call(
        functools.partial(select_kernel, partners, hslot),
        out_shape=shapes,
        interpret=INTERPRET,
        name="gather_send",
    )(slots, values)
    return outs[:groups], outs[groups]


def local_kernel(values_ref, local_ref, mixing_ref, out_ref):
    levels = values_ref.shape[0]
    for level in range(levels):
        v = values_ref[level]
        x = v + jnp.dot(
            v, local_ref[level], precision=HIGH, preferred_element_type=jnp.float32
        )
        if level + 1 < levels:
            x = x + mixing_ref[level : level + 1, :] * (values_ref[level + 1] - v)
        if level > 0:
            x = x - mixing_ref[level - 1 : level, :] * (v - values_ref[level - 1])
        out_ref[level] = x


def local_part(values, matrix, mixing):
    levels, pulses, capacity = values.shape
    pb = pulses // PULSE_BLOCKS if pulses % (8 * PULSE_BLOCKS) == 0 else pulses
    value_spec = pl.BlockSpec((levels, pb, capacity), lambda i: (0, i, 0))
    return pl.pallas_call(
        local_kernel,
        out_shape=jax.ShapeDtypeStruct(values.shape, jnp.float32),
        grid=(pulses // pb,),
        in_specs=[
            value_spec,
            pl.BlockSpec((levels, capacity, capacity), lambda i: (0, 0, 0)),
            full_spec(mixing.shape),
        ],
        out_specs=value_spec,
        interpret=INTERPRET,
        name="local_part",
    )(values, matrix, mixing)


def finish_kernel(groups, hslot, send, *refs):
    partial_ref = refs[0]
    incoming = refs[1 : 1 + groups]
    remote_refs = refs[1 + groups : 1 + 2 * groups]
    deposition_ref, count_ref, select_ref = refs[1 + 2 * groups : 4 + 2 * groups]
    out_ref = refs[4 + 2 * groups]
    send_refs = refs[5 + 2 * groups :]
    lb = partial_ref.shape[0]
    first = 0
    capacity = partial_ref.shape[2]
    living = lax.broadcasted_iota(jnp.int32, (1, capacity), 1) < count_ref[...]
    for level in range(lb):
        received = jnp.concatenate([incoming[g][level] for g in range(groups)], axis=0)
        weights = jnp.concatenate([remote_refs[g][level] for g in range(groups)], axis=0)
        far = lax.dot_general(
            received,
            weights,
            TN,
            precision=HIGH,
            preferred_element_type=jnp.float32,
        )
        keep = 1.0 - deposition_ref[first + level : first + level + 1, :]
        x = (partial_ref[level] + far) * keep
        x = jnp.where(living, x, 0.0)
        out_ref[level] = x
        if send:
            block = lax.dot_general(
                select_ref[...], x, NT, precision=HIGH, preferred_element_type=jnp.float32
            )
            for g in range(groups):
                send_refs[g][level] = block[g * hslot : (g + 1) * hslot]


def finish(partial, incoming, matrix, deposition, count, select, send):
    levels, pulses, capacity = partial.shape
    groups = len(incoming)
    hslot = incoming[0].shape[1]
    shapes = [jax.ShapeDtypeStruct(partial.shape, jnp.float32)]
    if send:
        shapes += [jax.ShapeDtypeStruct((levels, hslot, pulses), jnp.float32)] * groups
    operands = [partial, *incoming, *([matrix] * groups), deposition, count, select]
    specs = [full_spec(x.shape) for x in operands]
    for g in range(groups):
        block = capacity // hslot + g
        specs[1 + groups + g] = pl.BlockSpec(
            (levels, hslot, capacity), lambda i, block=block: (0, block, 0)
        )
    outs = pl.pallas_call(
        functools.partial(finish_kernel, groups, hslot, send),
        out_shape=shapes,
        grid=(1,),
        in_specs=specs,
        out_specs=[full_spec(x.shape) for x in shapes],
        interpret=INTERPRET,
        name="finish_send" if send else "finish",
    )(*operands)
    return outs[0], outs[1:]


def per_device(
    n, concentration, flux_weight, vertical_mixing, deposition, halo_index, send_cells, live_count
):
    levels, pulses, capacity = concentration.shape
    hslot = send_cells.shape[2]
    nbr = flux_weight.shape[0]
    partners = pairings(n)
    groups = len(partners)
    me = lax.axis_index("cells")
    f32 = jnp.float32

    lanes = jnp.arange(capacity, dtype=jnp.int32)
    values = concentration
    outgoing, select = gather_send(values, send_cells[0].T, partners, hslot)

    beyond = halo_index - capacity
    sender = beyond // hslot
    place = beyond % hslot
    row = jnp.where(beyond < 0, halo_index, -1)
    for g, partner in enumerate(partners):
        row = jnp.where(
            (beyond >= 0) & (sender == partner(me, jnp)), capacity + g * hslot + place, row
        )
    slots = jnp.arange(capacity + groups * hslot, dtype=jnp.int32)[:, None]
    diagonal = (slots == lanes[None, :]).astype(f32)
    matrix = sum(
        flux_weight[k][:, None, :] * ((row[k][None, :] == slots).astype(f32) - diagonal)[None]
        for k in range(nbr)
    )
    count = live_count.reshape(1, 1)

    for sweep in range(STEPS):
        incoming = [
            lax.ppermute(outgoing[g], "cells", perm=pair_list(n, partner))
            for g, partner in enumerate(partners)
        ]
        partial = local_part(values, matrix, vertical_mixing)
        values, outgoing = finish(
            partial, incoming, matrix, deposition, count, select, sweep + 1 < STEPS
        )
    return values


def solution(mesh):
    n = mesh.shape["cells"]
    in_specs = (
        P(None, None, "cells"),
        P(None, None, "cells"),
        P(None, "cells"),
        P(None, "cells"),
        P(None, "cells"),
        P("cells", None, None),
        P("cells"),
    )
    out_specs = P(None, None, "cells")

    def body(*args):
        return per_device(n, *args)

    return jax.shard_map(body, mesh=mesh, in_specs=in_specs, out_specs=out_specs, check_vma=False)
```
